32 devices in a mesh: clips: 2 (over y), frames: 4 (over z), wshard: 4 (over x, core).
Axes of the slice: x: 2, y: 2, z: 4, core: 2. Of those that a mesh axis runs over, the one named last changes fastest.
Arguments:
- tokens: bfloat16 [6144, 5120], P(('clips', 'frames')), parts along dimension 0, may hold values from -17 to 17
- w_query: bfloat16 [5120, 3072], P('frames', 'wshard'), may hold values from -0.08385255 to 0.08385255
- w_key: bfloat16 [5120, 3072], P('frames', 'wshard'), may hold values from -0.08385255 to 0.08385255
- w_value: bfloat16 [5120, 3072], P('frames', 'wshard'), may hold values from -0.078125 to 0.078125
- q_gain: float32 [3072], P('wshard'), may hold values from 0.4 to 7
- k_gain: float32 [3072], P('wshard'), may hold values from 0.4 to 7
- w_out: bfloat16 [3072, 5120], P('frames', 'wshard'), may hold values from -0.109375 to 0.109375
- key_blocks: int32 [48, 8], P(('clips', 'frames')), parts along dimension 0, may hold values from 0 to 17, as said below
- slab_counts: int32 [8], P('clips'), parts along dimension 0, may hold values from 384 to 768, as said below
Outputs:
- mixed: bfloat16 [6144, 5120], P(('clips', 'frames'), 'wshard'), parts along dimension 0
The draws below stay inside these ranges and needn't reach their ends.
There are 2 independent parts, one for each index of `clips`. The reference program is written for one: setup_inputs(seed, part) draws one part's arguments, and reference() takes and returns one part's arrays. A program takes and returns all parts, laid end to end along the dimension named above; an argument that names none is the same for every part. Nothing has to cross between parts.
Inputs may be any that keep to these rules, and one draw needn't show every extreme that they name: `key_blocks`: each row names 8 different blocks of its window, among them the query's own block, number 6 + i for block i of a slab. `slab_counts`: some slab is full in every clip.
All inputs are finite; a program needn't handle non-finite values.
Results may differ from the reference program's by a relative error of at most 0.0085.
Values may be sent and summed in bfloat16 or wider, within the bound.
No kernel may reach another device: no remote copies, remote signals or barrier semaphores. Data moves between devices by JAX's collectives and lax.ppermute only.
A program may use at most 192 MiB of HBM per device.

```python
import math
import jax
import jax.numpy as jnp
from jax import lax

D = 5120
HEAD_DIM = 128
TILE = 128
NB = 8
TOK_DEV = 768
HD = 3072
TILES = 6
TOKENS = 3072


def draw_tokens(key, part):
    first = jax.random.fold_in(jax.random.fold_in(key, 3), 0)
    return jnp.clip(jax.random.normal(first, (TOKENS, D)), -6.0, 6.0).astype(jnp.bfloat16)


def base_weight(key):
    return jnp.clip(jax.random.normal(jax.random.fold_in(key, 31), (D, HD)), -6.0, 6.0) * D ** (-0.5)


def draw_w_query(key, part):
    return base_weight(key).astype(jnp.bfloat16)


def draw_w_key(key, part):
    other = jnp.clip(jax.random.normal(jax.random.fold_in(key, 32), (D, HD)), -6.0, 6.0) * D ** (-0.5)
    return other.astype(jnp.bfloat16)


def draw_gain(key, salt):
    return jnp.exp(jax.random.uniform(jax.random.fold_in(key, salt), (HD,), minval=math.log(0.5), maxval=math.log(2.0))).astype(jnp.float32)


def draw_q_gain(key, part):
    return draw_gain(key, 22)


def draw_k_gain(key, part):
    return draw_gain(key, 23)


def draw_key_blocks(key, part):
    block_rows = TOKENS // TILE
    window = 3 * TILES
    raw = jax.random.randint(jax.random.fold_in(key, 41), (block_rows, window), 0, 65536)
    columns = jnp.arange(window, dtype=jnp.int32)[None, :]
    scores = raw * 128 + columns
    own = TILES + jnp.arange(block_rows, dtype=jnp.int32) % TILES
    scores = jnp.where(columns == own[:, None], 268435456, scores)
    return lax.top_k(scores, NB)[1].astype(jnp.int32)


def draw_slab_counts(key, part):
    slabs = TOKENS // TOK_DEV
    counts = jax.random.randint(jax.random.fold_in(key, 51), (slabs,), TOK_DEV // 2, TOK_DEV + 1)
    chosen = jax.random.randint(jax.random.fold_in(key, 52), (), 0, slabs)
    return jnp.where(jnp.arange(slabs) == chosen, TOK_DEV, counts).astype(jnp.int32)


def levels(rng, extent, cuts, least, largest):
    level = 1.0
    for axis_at, blocks in cuts:
        steps = jax.random.uniform(jax.random.fold_in(jax.random.fold_in(rng, 6), axis_at), (blocks,), jnp.float32, least / len(cuts), largest / len(cuts))
        level = level * jnp.repeat(jnp.exp(steps), extent[axis_at] // blocks).reshape((-1,) + (1,) * (len(extent) - 1 - axis_at))
    return level


def gaussian(rng, dims, scale, most, cuts=(), kind=jnp.bfloat16):
    values = jax.random.normal(rng, dims, jnp.float32) * scale
    if len(cuts) > 0:
        values = levels(rng, dims, cuts, -0.22, 0.18) * values
    return jnp.clip(values, min=-most, max=most).astype(kind)


def setup_inputs(seed: int = 0, part: int = 0) -> dict:
    seeds = jax.random.split(jax.random.key(seed), 10)
    own_keys = jax.random.split(jax.random.fold_in(seeds[9], part), 10)
    tokens = draw_tokens(jax.random.fold_in(jax.random.fold_in(seeds[9], part), 71), part)
    w_query = draw_w_query(jax.random.fold_in(seeds[9], 71), part)
    w_key = draw_w_key(jax.random.fold_in(seeds[9], 71), part)
    w_value = gaussian(seeds[3], (D, HD), D ** -0.5, 0.078125, ((0, 4), (1, 4)))
    q_gain = draw_q_gain(jax.random.fold_in(seeds[9], 71), part)
    k_gain = draw_k_gain(jax.random.fold_in(seeds[9], 71), part)
    w_out = gaussian(seeds[6], (HD, D), HD ** -0.5, 0.109375, ((0, 4), (1, 4)))
    key_blocks = draw_key_blocks(jax.random.fold_in(jax.random.fold_in(seeds[9], part), 71), part)
    slab_counts = draw_slab_counts(jax.random.fold_in(jax.random.fold_in(seeds[9], part), 71), part)
    return {"tokens": tokens, "w_query": w_query, "w_key": w_key, "w_value": w_value, "q_gain": q_gain, "k_gain": k_gain, "w_out": w_out, "key_blocks": key_blocks, "slab_counts": slab_counts}


def head_norm(raw, gain):
    rows, cols = raw.shape
    split = raw.reshape(rows, cols // HEAD_DIM, HEAD_DIM)
    square = lax.optimization_barrier(jnp.mean(split * split, axis=-1, keepdims=True))
    normed = (split * lax.rsqrt(square + 1e-06)).reshape(rows, cols)
    return (normed * gain).astype(jnp.bfloat16)

def attend(query, keys, values, blocks, limits):
    rows, cols = query.shape
    tiles = rows // TILE
    heads = cols // HEAD_DIM
    picks = blocks.shape[1]
    window = keys.shape[0] // TILE
    key_tiles = keys.reshape(window, TILE, cols)[blocks].reshape(tiles, picks * TILE, heads, HEAD_DIM)
    value_tiles = values.reshape(window, TILE, cols)[blocks].reshape(tiles, picks * TILE, heads, HEAD_DIM)
    tile_ids = jnp.arange(window, dtype=jnp.int32)
    slab_of = tile_ids // tiles
    limit = jnp.where(slab_of == 0, limits[0], jnp.where(slab_of == 1, limits[1], limits[2]))
    offsets = (tile_ids % tiles)[:, None] * TILE + jnp.arange(TILE, dtype=jnp.int32)[None, :]
    live = offsets < limit[:, None]
    live_keys = live[blocks].reshape(tiles, picks * TILE)
    query_tiles = query.reshape(tiles, TILE, heads, HEAD_DIM)
    scores = jnp.einsum('iqhd,ikhd->ihqk', query_tiles.astype(jnp.float32), key_tiles.astype(jnp.float32))
    scores = scores * (1.0 / math.sqrt(HEAD_DIM))
    scores = jnp.where(live_keys[:, None, None, :], scores, -1e+30)
    top = lax.optimization_barrier(jnp.max(scores, axis=-1, keepdims=True))
    expo = jnp.exp(scores - top)
    weights = (expo / lax.optimization_barrier(jnp.sum(expo, axis=-1, keepdims=True))).astype(jnp.bfloat16)
    mixed = jnp.einsum('ihqk,ikhd->iqhd', weights.astype(jnp.float32), value_tiles.astype(jnp.float32))
    mixed = mixed.reshape(rows, cols)
    own_rows = jnp.arange(rows, dtype=jnp.int32) < limits[1]
    return jnp.where(own_rows[:, None], mixed, 0.0).astype(jnp.bfloat16)

def reference(tokens, w_query, w_key, w_value, q_gain, k_gain, w_out, key_blocks, slab_counts):
    slabs = TOKENS // TOK_DEV
    query = head_norm(jnp.dot(tokens, w_query, preferred_element_type=jnp.float32), q_gain)
    keys = head_norm(jnp.dot(tokens, w_key, preferred_element_type=jnp.float32), k_gain)
    values = jnp.dot(tokens, w_value, preferred_element_type=jnp.float32).astype(jnp.bfloat16)
    empty = jnp.zeros((1, TOK_DEV, HD), jnp.bfloat16)
    key_pad = jnp.concatenate([empty, keys.reshape(slabs, TOK_DEV, HD), empty], axis=0)
    value_pad = jnp.concatenate([empty, values.reshape(slabs, TOK_DEV, HD), empty], axis=0)
    zero = jnp.zeros((1,), jnp.int32)
    count_pad = jnp.concatenate([zero, slab_counts.astype(jnp.int32), zero], axis=0)
    query_slabs = query.reshape(slabs, TOK_DEV, HD)
    block_slabs = key_blocks.reshape(slabs, TILES, NB)

    def one_slab(slab):
        key_window = lax.dynamic_slice_in_dim(key_pad, slab, 3, 0).reshape(3 * TOK_DEV, HD)
        value_window = lax.dynamic_slice_in_dim(value_pad, slab, 3, 0).reshape(3 * TOK_DEV, HD)
        limits = lax.dynamic_slice_in_dim(count_pad, slab, 3, 0)
        return attend(query_slabs[slab], key_window, value_window, block_slabs[slab], limits)
    attended = lax.map(one_slab, jnp.arange(slabs, dtype=jnp.int32)).reshape(TOKENS, HD)
    return jnp.dot(attended, w_out, preferred_element_type=jnp.float32).astype(jnp.bfloat16)
```

```python
import math

import jax
import jax.numpy as jnp
from jax import lax
from jax.sharding import PartitionSpec as P

HEAD_DIM = 128
TILE = 128


def shifted(value, axis, by):
    size = lax.axis_size(axis)
    pairs = [(i, i + by) for i in range(size) if 0 <= i + by < size]
    return lax.ppermute(value, axis, pairs)


def head_norm(raw, gain):
    rows, cols = raw.shape
    split = raw.reshape(rows, cols // HEAD_DIM, HEAD_DIM)
    square = jnp.mean(split * split, axis=-1, keepdims=True)
    normed = (split * lax.rsqrt(square + 1e-06)).reshape(rows, cols)
    return (normed * gain).astype(jnp.bfloat16)


def attend(query, keys, values, blocks, limits):
    rows, cols = query.shape
    tiles = rows // TILE
    heads = cols // HEAD_DIM
    picks = blocks.shape[1]
    window = keys.shape[0] // TILE
    key_tiles = keys.reshape(window, TILE, cols)[blocks].reshape(
        tiles, picks * TILE, heads, HEAD_DIM
    )
    value_tiles = values.reshape(window, TILE, cols)[blocks].reshape(
        tiles, picks * TILE, heads, HEAD_DIM
    )
    tile_ids = jnp.arange(window, dtype=jnp.int32)
    slab_of = tile_ids // tiles
    limit = jnp.where(slab_of == 0, limits[0], jnp.where(slab_of == 1, limits[1], limits[2]))
    offsets = (tile_ids % tiles)[:, None] * TILE + jnp.arange(TILE, dtype=jnp.int32)[None, :]
    live = offsets < limit[:, None]
    live_keys = live[blocks].reshape(tiles, picks * TILE)
    query_tiles = query.reshape(tiles, TILE, heads, HEAD_DIM)
    scores = jnp.einsum(
        "iqhd,ikhd->ihqk", query_tiles, key_tiles, preferred_element_type=jnp.float32
    )
    scores = scores * (1.0 / math.sqrt(HEAD_DIM))
    scores = jnp.where(live_keys[:, None, None, :], scores, -1e30)
    top = jnp.max(scores, axis=-1, keepdims=True)
    expo = jnp.exp(scores - top)
    weights = (expo / jnp.sum(expo, axis=-1, keepdims=True)).astype(jnp.bfloat16)
    mixed = jnp.einsum("ihqk,ikhd->iqhd", weights, value_tiles, preferred_element_type=jnp.float32)
    mixed = mixed.reshape(rows, cols)
    own_rows = jnp.arange(rows, dtype=jnp.int32) < limits[1]
    return jnp.where(own_rows[:, None], mixed, 0.0).astype(jnp.bfloat16)


def gather_rows(piece):
    parts = lax.axis_size("clips")
    share = piece.shape[0] // parts
    mine = lax.dynamic_slice_in_dim(piece, lax.axis_index("clips") * share, share, 0)
    return lax.all_gather(mine, ("frames", "clips"), axis=0, tiled=True)


def per_device(tokens, w_query, w_key, w_value, q_gain, k_gain, w_out, key_blocks, slab_counts):

    def project(piece):
        return jnp.dot(tokens, piece, preferred_element_type=jnp.float32)

    query_raw = project(gather_rows(w_query))
    key_raw = project(gather_rows(w_key))
    value_raw = project(gather_rows(w_value))
    query = head_norm(query_raw, q_gain)
    keys = head_norm(key_raw, k_gain)
    values = value_raw.astype(jnp.bfloat16)
    before = shifted((keys, values), "frames", 1)
    after = shifted((keys, values), "frames", -1)
    key_window = jnp.concatenate([before[0], keys, after[0]], axis=0)
    value_window = jnp.concatenate([before[1], values, after[1]], axis=0)
    position = lax.axis_index("frames")
    zero = jnp.zeros((1,), jnp.int32)
    count_pad = jnp.concatenate([zero, slab_counts, zero], axis=0)
    limits = lax.dynamic_slice_in_dim(count_pad, position, 3, 0)
    attended = attend(query, key_window, value_window, key_blocks, limits)
    whole = lax.all_gather(attended, "wshard", axis=1, tiled=True)
    mixed = jnp.dot(
        whole,
        gather_rows(w_out),
        preferred_element_type=jnp.float32,
    )
    return mixed.astype(jnp.bfloat16)


def solution(mesh):
    return jax.shard_map(
        per_device,
        mesh=mesh,
        in_specs=(
            P(("clips", "frames"), None),
            P("frames", "wshard"),
            P("frames", "wshard"),
            P("frames", "wshard"),
            P("wshard"),
            P("wshard"),
            P("frames", "wshard"),
            P(("clips", "frames"), None),
            P("clips"),
        ),
        out_specs=P(("clips", "frames"), "wshard"),
        check_vma=False,
    )
```

```python
import math

import jax
import jax.numpy as jnp
from jax import lax
from jax.sharding import PartitionSpec as P

HEAD_DIM = 128
TILE = 128


def shifted(value, axis, by):
    size = lax.axis_size(axis)
    pairs = [(i, i + by) for i in range(size) if 0 <= i + by < size]
    return lax.ppermute(value, axis, pairs)


def head_norm(raw, gain):
    rows, cols = raw.shape
    split = raw.reshape(rows, cols // HEAD_DIM, HEAD_DIM)
    square = jnp.mean(split * split, axis=-1, keepdims=True)
    normed = (split * lax.rsqrt(square + 1e-06)).reshape(rows, cols)
    return (normed * gain).astype(jnp.bfloat16)


def attend(query, keys, values, blocks, limits):
    rows, cols = query.shape
    tiles = rows // TILE
    heads = cols // HEAD_DIM
    picks = blocks.shape[1]
    window = keys.shape[0] // TILE
    key_tiles = keys.reshape(window, TILE, cols)[blocks].reshape(
        tiles, picks * TILE, heads, HEAD_DIM
    )
    value_tiles = values.reshape(window, TILE, cols)[blocks].reshape(
        tiles, picks * TILE, heads, HEAD_DIM
    )
    tile_ids = jnp.arange(window, dtype=jnp.int32)
    slab_of = tile_ids // tiles
    limit = jnp.where(slab_of == 0, limits[0], jnp.where(slab_of == 1, limits[1], limits[2]))
    offsets = (tile_ids % tiles)[:, None] * TILE + jnp.arange(TILE, dtype=jnp.int32)[None, :]
    live = offsets < limit[:, None]
    live_keys = live[blocks].reshape(tiles, picks * TILE)
    query_tiles = query.reshape(tiles, TILE, heads, HEAD_DIM)
    scores = jnp.einsum(
        "iqhd,ikhd->ihqk", query_tiles, key_tiles, preferred_element_type=jnp.float32
    )
    scores = scores * (1.0 / math.sqrt(HEAD_DIM))
    scores = jnp.where(live_keys[:, None, None, :], scores, -1e30)
    top = jnp.max(scores, axis=-1, keepdims=True)
    expo = jnp.exp(scores - top)
    weights = (expo / jnp.sum(expo, axis=-1, keepdims=True)).astype(jnp.bfloat16)
    mixed = jnp.einsum("ihqk,ikhd->iqhd", weights, value_tiles, preferred_element_type=jnp.float32)
    mixed = mixed.reshape(rows, cols)
    own_rows = jnp.arange(rows, dtype=jnp.int32) < limits[1]
    return jnp.where(own_rows[:, None], mixed, 0.0).astype(jnp.bfloat16)


def split_gather(piece):
    parts = lax.axis_size("clips")
    chunks = lax.axis_size("frames")
    assert parts == 2
    ci = lax.axis_index("clips")
    fi = lax.axis_index("frames")
    rows, cols = piece.shape
    share = rows // parts
    halves = piece.reshape(parts, share, cols)
    mine = lax.dynamic_index_in_dim(halves, ci, 0, keepdims=False)
    other = lax.dynamic_index_in_dim(halves, 1 - ci, 0, keepdims=False)
    got = lax.all_gather(mine, "frames", axis=0, tiled=False)
    foreign = jnp.arange(chunks - 1, dtype=jnp.int32)
    foreign = foreign + (foreign >= fi).astype(jnp.int32)
    sent = got[foreign]
    recv = lax.ppermute(sent, "clips", [(0, 1), (1, 0)])
    return (
        got.reshape(chunks * share, cols),
        recv.reshape((chunks - 1) * share, cols),
        other,
    ), (ci, fi, foreign)


def split_cols(x, share, where):
    ci, fi, foreign = where
    n, width = x.shape
    parts = 2
    chunks = width // (parts * share)
    blocks = x.reshape(n, chunks, parts, share)
    mine = lax.dynamic_index_in_dim(blocks, ci, 2, keepdims=False)
    other = lax.dynamic_index_in_dim(blocks, 1 - ci, 2, keepdims=False)
    return (
        mine.reshape(n, chunks * share),
        other[:, foreign].reshape(n, (chunks - 1) * share),
        lax.dynamic_index_in_dim(other, fi, 1, keepdims=False),
    )


def split_dot(cols, rows):
    total = None
    for a, b in zip(cols, rows):
        part = jnp.dot(a, b, preferred_element_type=jnp.float32)
        total = part if total is None else total + part
    return total


def per_device(tokens, w_query, w_key, w_value, q_gain, k_gain, w_out, key_blocks, slab_counts):
    share = w_query.shape[0] // lax.axis_size("clips")
    k_rows, where = split_gather(w_key)
    v_rows, _ = split_gather(w_value)
    q_rows, _ = split_gather(w_query)
    o_rows, _ = split_gather(w_out)
    token_cols = split_cols(tokens, share, where)
    query = head_norm(split_dot(token_cols, q_rows), q_gain)
    keys = head_norm(split_dot(token_cols, k_rows), k_gain)
    values = split_dot(token_cols, v_rows).astype(jnp.bfloat16)
    before = shifted((keys, values), "frames", 1)
    after = shifted((keys, values), "frames", -1)
    key_window = jnp.concatenate([before[0], keys, after[0]], axis=0)
    value_window = jnp.concatenate([before[1], values, after[1]], axis=0)
    position = lax.axis_index("frames")
    zero = jnp.zeros((1,), jnp.int32)
    count_pad = jnp.concatenate([zero, slab_counts, zero], axis=0)
    limits = lax.dynamic_slice_in_dim(count_pad, position, 3, 0)
    attended = attend(query, key_window, value_window, key_blocks, limits)
    whole = lax.all_gather(attended, "wshard", axis=1, tiled=True)
    out_share = w_out.shape[0] // lax.axis_size("clips")
    mixed = split_dot(split_cols(whole, out_share, where), o_rows)
    return mixed.astype(jnp.bfloat16)


def solution(mesh):
    return jax.shard_map(
        per_device,
        mesh=mesh,
        in_specs=(
            P(("clips", "frames"), None),
            P("frames", "wshard"),
            P("frames", "wshard"),
            P("frames", "wshard"),
            P("wshard"),
            P("wshard"),
            P("frames", "wshard"),
            P(("clips", "frames"), None),
            P("clips"),
        ),
        out_specs=P(("clips", "frames"), "wshard"),
        check_vma=False,
    )
```

```python
import math

import jax
import jax.numpy as jnp
from jax import lax
from jax.experimental import pallas as pl
from jax.experimental.pallas import tpu as pltpu
from jax.sharding import PartitionSpec as P

HEAD_DIM = 128
TILE = 128


def shifted(value, axis, by):
    size = lax.axis_size(axis)
    pairs = [(i, i + by) for i in range(size) if 0 <= i + by < size]
    return lax.ppermute(value, axis, pairs)


def head_norm(raw, gain):
    rows, cols = raw.shape
    split = raw.reshape(rows, cols // HEAD_DIM, HEAD_DIM)
    square = jnp.mean(split * split, axis=-1, keepdims=True)
    normed = (split * lax.rsqrt(square + 1e-06)).reshape(rows, cols)
    return (normed * gain).astype(jnp.bfloat16)


def attend_kernel(kb_ref, lim_ref, q_ref, k_ref, v_ref, o_ref):
    tiles = q_ref.shape[0] // TILE
    picks = kb_ref.shape[1]
    scale = 1.0 / math.sqrt(HEAD_DIM)
    lanes = lax.broadcasted_iota(jnp.int32, (TILE, TILE), 1)
    rows = lax.broadcasted_iota(jnp.int32, (TILE, TILE), 0)

    def one_tile(i, carry):
        start = pl.multiple_of(i * TILE, TILE)
        q = q_ref[pl.ds(start, TILE), :]
        scores = []
        for j in range(picks):
            b = kb_ref[i, j]
            k = k_ref[pl.ds(pl.multiple_of(b * TILE, TILE), TILE), :]
            s = lax.dot_general(
                q, k, (((1,), (1,)), ((), ())), preferred_element_type=jnp.float32
            )
            s = s * scale
            slab = (b >= tiles).astype(jnp.int32) + (b >= 2 * tiles).astype(jnp.int32)
            limit = lim_ref[slab]
            pos = (b - slab * tiles) * TILE + lanes
            scores.append(jnp.where(pos < limit, s, -1e30))
        top = jnp.max(scores[0], axis=1, keepdims=True)
        for s in scores[1:]:
            top = jnp.maximum(top, jnp.max(s, axis=1, keepdims=True))
        expo = [jnp.exp(s - top) for s in scores]
        total = jnp.sum(expo[0], axis=1, keepdims=True)
        for e in expo[1:]:
            total = total + jnp.sum(e, axis=1, keepdims=True)
        acc = None
        for j in range(picks):
            b = kb_ref[i, j]
            v = v_ref[pl.ds(pl.multiple_of(b * TILE, TILE), TILE), :]
            w = (expo[j] / total).astype(jnp.bfloat16)
            part = jnp.dot(w, v, preferred_element_type=jnp.float32)
            acc = part if acc is None else acc + part
        live = start + rows < lim_ref[1]
        o_ref[pl.ds(start, TILE), :] = jnp.where(live, acc, 0.0).astype(o_ref.dtype)
        return carry

    lax.fori_loop(0, tiles, one_tile, 0)


def attend(query, keys, values, blocks, limits, interpret=False):
    rows, cols = query.shape
    window = keys.shape[0]
    heads = cols // HEAD_DIM
    spec = pltpu.PrefetchScalarGridSpec(
        num_scalar_prefetch=2,
        grid=(heads,),
        in_specs=[
            pl.BlockSpec((rows, HEAD_DIM), lambda h, kb, lim: (0, h)),
            pl.BlockSpec((window, HEAD_DIM), lambda h, kb, lim: (0, h)),
            pl.BlockSpec((window, HEAD_DIM), lambda h, kb, lim: (0, h)),
        ],
        out_specs=pl.BlockSpec((rows, HEAD_DIM), lambda h, kb, lim: (0, h)),
    )
    return pl.pallas_call(
        attend_kernel,
        grid_spec=spec,
        out_shape=jax.ShapeDtypeStruct((rows, cols), jnp.bfloat16),
        interpret=interpret,
    )(blocks.astype(jnp.int32), limits.astype(jnp.int32), query, keys, values)


def split_gather(piece):
    parts = lax.axis_size("clips")
    chunks = lax.axis_size("frames")
    assert parts == 2
    ci = lax.axis_index("clips")
    fi = lax.axis_index("frames")
    rows, cols = piece.shape
    share = rows // parts
    halves = piece.reshape(parts, share, cols)
    mine = lax.dynamic_index_in_dim(halves, ci, 0, keepdims=False)
    other = lax.dynamic_index_in_dim(halves, 1 - ci, 0, keepdims=False)
    got = lax.all_gather(mine, "frames", axis=0, tiled=False)
    foreign = jnp.arange(chunks - 1, dtype=jnp.int32)
    foreign = foreign + (foreign >= fi).astype(jnp.int32)
    sent = got[foreign]
    recv = lax.ppermute(sent, "clips", [(0, 1), (1, 0)])
    return (
        got.reshape(chunks * share, cols),
        recv.reshape((chunks - 1) * share, cols),
        other,
    ), (ci, fi, foreign)


def split_cols(x, share, where):
    ci, fi, foreign = where
    n, width = x.shape
    parts = 2
    chunks = width // (parts * share)
    blocks = x.reshape(n, chunks, parts, share)
    mine = lax.dynamic_index_in_dim(blocks, ci, 2, keepdims=False)
    other = lax.dynamic_index_in_dim(blocks, 1 - ci, 2, keepdims=False)
    return (
        mine.reshape(n, chunks * share),
        other[:, foreign].reshape(n, (chunks - 1) * share),
        lax.dynamic_index_in_dim(other, fi, 1, keepdims=False),
    )


def split_dot(cols, rows):
    total = None
    for a, b in zip(cols, rows):
        part = jnp.dot(a, b, preferred_element_type=jnp.float32)
        total = part if total is None else total + part
    return total


def per_device(tokens, w_query, w_key, w_value, q_gain, k_gain, w_out, key_blocks, slab_counts):
    share = w_query.shape[0] // lax.axis_size("clips")
    k_rows, where = split_gather(w_key)
    v_rows, _ = split_gather(w_value)
    q_rows, _ = split_gather(w_query)
    o_rows, _ = split_gather(w_out)
    token_cols = split_cols(tokens, share, where)
    query = head_norm(split_dot(token_cols, q_rows), q_gain)
    keys = head_norm(split_dot(token_cols, k_rows), k_gain)
    values = split_dot(token_cols, v_rows).astype(jnp.bfloat16)
    before = shifted((keys, values), "frames", 1)
    after = shifted((keys, values), "frames", -1)
    key_window = jnp.concatenate([before[0], keys, after[0]], axis=0)
    value_window = jnp.concatenate([before[1], values, after[1]], axis=0)
    position = lax.axis_index("frames")
    zero = jnp.zeros((1,), jnp.int32)
    count_pad = jnp.concatenate([zero, slab_counts, zero], axis=0)
    limits = lax.dynamic_slice_in_dim(count_pad, position, 3, 0)
    attended = attend(query, key_window, value_window, key_blocks, limits)
    whole = lax.all_gather(attended, "wshard", axis=1, tiled=True)
    out_share = w_out.shape[0] // lax.axis_size("clips")
    mixed = split_dot(split_cols(whole, out_share, where), o_rows)
    return mixed.astype(jnp.bfloat16)


def solution(mesh):
    return jax.shard_map(
        per_device,
        mesh=mesh,
        in_specs=(
            P(("clips", "frames"), None),
            P("frames", "wshard"),
            P("frames", "wshard"),
            P("frames", "wshard"),
            P("wshard"),
            P("wshard"),
            P("frames", "wshard"),
            P(("clips", "frames"), None),
            P("clips"),
        ),
        out_specs=P(("clips", "frames"), "wshard"),
        check_vma=False,
    )
```

```python
import math

import jax
import jax.numpy as jnp
from jax import lax
from jax.experimental import pallas as pl
from jax.experimental.pallas import tpu as pltpu
from jax.sharding import PartitionSpec as P

HEAD_DIM = 128
TILE = 128


def shifted(value, axis, by):
    size = lax.axis_size(axis)
    pairs = [(i, i + by) for i in range(size) if 0 <= i + by < size]
    return lax.ppermute(value, axis, pairs)


def head_norm(raw, gain):
    rows, cols = raw.shape
    split = raw.reshape(rows, cols // HEAD_DIM, HEAD_DIM)
    square = jnp.mean(split * split, axis=-1, keepdims=True)
    normed = (split * lax.rsqrt(square + 1e-06)).reshape(rows, cols)
    return (normed * gain).astype(jnp.bfloat16)


def attend_kernel(kb_ref, lim_ref, q_ref, k_ref, v_ref, o_ref):
    tiles = q_ref.shape[0] // TILE
    picks = kb_ref.shape[1]
    scale = 1.0 / math.sqrt(HEAD_DIM)
    lanes = lax.broadcasted_iota(jnp.int32, (TILE, TILE), 1)
    rows = lax.broadcasted_iota(jnp.int32, (TILE, TILE), 0)

    def one_tile(i, carry):
        start = pl.multiple_of(i * TILE, TILE)
        q = q_ref[pl.ds(start, TILE), :]
        scores = []
        for j in range(picks):
            b = kb_ref[i, j]
            k = k_ref[pl.ds(pl.multiple_of(b * TILE, TILE), TILE), :]
            s = lax.dot_general(
                q, k, (((1,), (1,)), ((), ())), preferred_element_type=jnp.float32
            )
            s = s * scale
            slab = (b >= tiles).astype(jnp.int32) + (b >= 2 * tiles).astype(jnp.int32)
            limit = lim_ref[slab]
            pos = (b - slab * tiles) * TILE + lanes
            scores.append(jnp.where(pos < limit, s, -1e30))
        top = jnp.max(scores[0], axis=1, keepdims=True)
        for s in scores[1:]:
            top = jnp.maximum(top, jnp.max(s, axis=1, keepdims=True))
        expo = [jnp.exp(s - top) for s in scores]
        total = jnp.sum(expo[0], axis=1, keepdims=True)
        for e in expo[1:]:
            total = total + jnp.sum(e, axis=1, keepdims=True)
        acc = None
        for j in range(picks):
            b = kb_ref[i, j]
            v = v_ref[pl.ds(pl.multiple_of(b * TILE, TILE), TILE), :]
            w = (expo[j] / total).astype(jnp.bfloat16)
            part = jnp.dot(w, v, preferred_element_type=jnp.float32)
            acc = part if acc is None else acc + part
        live = start + rows < lim_ref[1]
        o_ref[pl.ds(start, TILE), :] = jnp.where(live, acc, 0.0).astype(o_ref.dtype)
        return carry

    lax.fori_loop(0, tiles, one_tile, 0)


def attend(query, keys, values, blocks, limits, interpret=False):
    rows, cols = query.shape
    window = keys.shape[0]
    heads = cols // HEAD_DIM
    spec = pltpu.PrefetchScalarGridSpec(
        num_scalar_prefetch=2,
        grid=(heads,),
        in_specs=[
            pl.BlockSpec((rows, HEAD_DIM), lambda h, kb, lim: (0, h)),
            pl.BlockSpec((window, HEAD_DIM), lambda h, kb, lim: (0, h)),
            pl.BlockSpec((window, HEAD_DIM), lambda h, kb, lim: (0, h)),
        ],
        out_specs=pl.BlockSpec((rows, HEAD_DIM), lambda h, kb, lim: (0, h)),
    )
    return pl.pallas_call(
        attend_kernel,
        grid_spec=spec,
        out_shape=jax.ShapeDtypeStruct((rows, cols), jnp.bfloat16),
        interpret=interpret,
    )(blocks.astype(jnp.int32), limits.astype(jnp.int32), query, keys, values)


def split_gather(piece):
    parts = lax.axis_size("clips")
    chunks = lax.axis_size("frames")
    assert parts == 2
    ci = lax.axis_index("clips")
    fi = lax.axis_index("frames")
    rows, cols = piece.shape
    share = cols // parts
    halves = piece.reshape(rows, parts, share)
    mine = lax.dynamic_index_in_dim(halves, ci, 1, keepdims=False)
    other = lax.dynamic_index_in_dim(halves, 1 - ci, 1, keepdims=False)
    got = lax.all_gather(mine, "frames", axis=0, tiled=False)
    order = jnp.arange(chunks, dtype=jnp.int32)
    foreign = order[: chunks - 1] + (order[: chunks - 1] >= fi).astype(jnp.int32)
    recv = lax.ppermute(got[foreign], "clips", [(0, 1), (1, 0)])
    slot = jnp.clip(order - (order > fi).astype(jnp.int32), 0, chunks - 2)
    whole_other = jnp.where((order == fi)[:, None, None], other[None], recv[slot])
    return got.reshape(chunks * rows, share), whole_other.reshape(chunks * rows, share)


def split_dot(x, pair):
    own = jnp.dot(x, pair[0], preferred_element_type=jnp.float32)
    rest = jnp.dot(x, pair[1], preferred_element_type=jnp.float32)
    first = lax.axis_index("clips") == 0
    return jnp.where(first, jnp.concatenate([own, rest], 1), jnp.concatenate([rest, own], 1))


def per_device(tokens, w_query, w_key, w_value, q_gain, k_gain, w_out, key_blocks, slab_counts):
    k_rows = split_gather(w_key)
    v_rows = split_gather(w_value)
    q_rows = split_gather(w_query)
    o_rows = split_gather(w_out)
    query = head_norm(split_dot(tokens, q_rows), q_gain)
    keys = head_norm(split_dot(tokens, k_rows), k_gain)
    values = split_dot(tokens, v_rows).astype(jnp.bfloat16)
    before = shifted((keys, values), "frames", 1)
    after = shifted((keys, values), "frames", -1)
    key_window = jnp.concatenate([before[0], keys, after[0]], axis=0)
    value_window = jnp.concatenate([before[1], values, after[1]], axis=0)
    position = lax.axis_index("frames")
    zero = jnp.zeros((1,), jnp.int32)
    count_pad = jnp.concatenate([zero, slab_counts, zero], axis=0)
    limits = lax.dynamic_slice_in_dim(count_pad, position, 3, 0)
    query, o_rows = lax.optimization_barrier((query, o_rows))
    attended = attend(query, key_window, value_window, key_blocks, limits)
    whole = lax.all_gather(attended, "wshard", axis=1, tiled=True)
    mixed = split_dot(whole, o_rows)
    return mixed.astype(jnp.bfloat16)


def solution(mesh):
    return jax.shard_map(
        per_device,
        mesh=mesh,
        in_specs=(
            P(("clips", "frames"), None),
            P("frames", "wshard"),
            P("frames", "wshard"),
            P("frames", "wshard"),
            P("wshard"),
            P("wshard"),
            P("frames", "wshard"),
            P(("clips", "frames"), None),
            P("clips"),
        ),
        out_specs=P(("clips", "frames"), "wshard"),
        check_vma=False,
    )
```

```python
import math

import jax
import jax.numpy as jnp
from jax import lax
from jax.experimental import pallas as pl
from jax.experimental.pallas import tpu as pltpu
from jax.sharding import PartitionSpec as P


HEAD_DIM = 128
TILE = 128


def shifted(value, axis, by):
    size = lax.axis_size(axis)
    pairs = [(i, i + by) for i in range(size) if 0 <= i + by < size]
    return lax.ppermute(value, axis, pairs)


def head_norm(raw, gain):
    rows, cols = raw.shape
    split = raw.reshape(rows, cols // HEAD_DIM, HEAD_DIM)
    square = jnp.mean(split * split, axis=-1, keepdims=True)
    normed = (split * lax.rsqrt(square + 1e-06)).reshape(rows, cols)
    return (normed * gain).astype(jnp.bfloat16)


def attend_kernel(kb_ref, lim_ref, q_ref, k_ref, v_ref, o_ref):
    tiles = q_ref.shape[0] // TILE
    picks = kb_ref.shape[1]
    scale = 1.0 / math.sqrt(HEAD_DIM)
    lanes = lax.broadcasted_iota(jnp.int32, (TILE, TILE), 1)
    rows = lax.broadcasted_iota(jnp.int32, (TILE, TILE), 0)

    def one_tile(i, carry):
        start = pl.multiple_of(i * TILE, TILE)
        q = q_ref[pl.ds(start, TILE), :]
        scores = []
        for j in range(picks):
            b = kb_ref[i, j]
            k = k_ref[pl.ds(pl.multiple_of(b * TILE, TILE), TILE), :]
            s = lax.dot_general(
                q, k, (((1,), (1,)), ((), ())), preferred_element_type=jnp.float32
            )
            s = s * scale
            slab = (b >= tiles).astype(jnp.int32) + (b >= 2 * tiles).astype(jnp.int32)
            limit = lim_ref[slab]
            pos = (b - slab * tiles) * TILE + lanes
            scores.append(jnp.where(pos < limit, s, -1e30))
        top = jnp.max(scores[0], axis=1, keepdims=True)
        for s in scores[1:]:
            top = jnp.maximum(top, jnp.max(s, axis=1, keepdims=True))
        expo = [jnp.exp(s - top) for s in scores]
        total = jnp.sum(expo[0], axis=1, keepdims=True)
        for e in expo[1:]:
            total = total + jnp.sum(e, axis=1, keepdims=True)
        acc = None
        for j in range(picks):
            b = kb_ref[i, j]
            v = v_ref[pl.ds(pl.multiple_of(b * TILE, TILE), TILE), :]
            w = (expo[j] / total).astype(jnp.bfloat16)
            part = jnp.dot(w, v, preferred_element_type=jnp.float32)
            acc = part if acc is None else acc + part
        live = start + rows < lim_ref[1]
        o_ref[pl.ds(start, TILE), :] = jnp.where(live, acc, 0.0).astype(o_ref.dtype)
        return carry

    lax.fori_loop(0, tiles, one_tile, 0)


def attend(query, keys, values, blocks, limits, interpret=False):
    rows, cols = query.shape
    window = keys.shape[0]
    heads = cols // HEAD_DIM
    spec = pltpu.PrefetchScalarGridSpec(
        num_scalar_prefetch=2,
        grid=(heads,),
        in_specs=[
            pl.BlockSpec((rows, HEAD_DIM), lambda h, kb, lim: (0, h)),
            pl.BlockSpec((window, HEAD_DIM), lambda h, kb, lim: (0, h)),
            pl.BlockSpec((window, HEAD_DIM), lambda h, kb, lim: (0, h)),
        ],
        out_specs=pl.BlockSpec((rows, HEAD_DIM), lambda h, kb, lim: (0, h)),
    )
    return pl.pallas_call(
        attend_kernel,
        grid_spec=spec,
        out_shape=jax.ShapeDtypeStruct((rows, cols), jnp.bfloat16),
        interpret=interpret,
    )(blocks.astype(jnp.int32), limits.astype(jnp.int32), query, keys, values)


def fetch(piece):
    parts = lax.axis_size("clips")
    assert parts == 2
    ci = lax.axis_index("clips")
    rows, cols = piece.shape
    halves = piece.reshape(rows, parts, cols // parts)
    mine = lax.dynamic_index_in_dim(halves, ci, 1, keepdims=False)
    other = lax.dynamic_index_in_dim(halves, 1 - ci, 1, keepdims=False)
    return lax.all_gather(mine, "frames", axis=0, tiled=False), other


def trade(fetched):
    got, other = fetched
    chunks, rows, share = got.shape
    fi = lax.axis_index("frames")
    order = jnp.arange(chunks, dtype=jnp.int32)
    foreign = order[: chunks - 1] + (order[: chunks - 1] >= fi).astype(jnp.int32)
    recv = lax.ppermute(got[foreign], "clips", [(0, 1), (1, 0)])
    slot = jnp.clip(order - (order > fi).astype(jnp.int32), 0, chunks - 2)
    whole_other = jnp.where((order == fi)[:, None, None], other[None], recv[slot])
    return got.reshape(chunks * rows, share), whole_other.reshape(chunks * rows, share)


def split_dot(x, pair):
    own = jnp.dot(x, pair[0], preferred_element_type=jnp.float32)
    rest = jnp.dot(x, pair[1], preferred_element_type=jnp.float32)
    first = lax.axis_index("clips") == 0
    return jnp.where(first, jnp.concatenate([own, rest], 1), jnp.concatenate([rest, own], 1))


def layer(tokens, w_query, w_key, w_value, q_gain, k_gain, w_out, key_blocks, slab_counts):
    k_got = fetch(w_key)
    v_got = fetch(w_value)
    q_got = fetch(w_query)
    o_got = fetch(w_out)
    keys = head_norm(split_dot(tokens, trade(k_got)), k_gain)
    values = split_dot(tokens, trade(v_got)).astype(jnp.bfloat16)
    keys, values, q_got = lax.optimization_barrier((keys, values, q_got))
    query = head_norm(split_dot(tokens, trade(q_got)), q_gain)
    keys, values, o_got = lax.optimization_barrier((keys, values, o_got))
    o_rows = trade(o_got)
    before = shifted((keys, values), "frames", 1)
    after = shifted((keys, values), "frames", -1)
    key_window = jnp.concatenate([before[0], keys, after[0]], axis=0)
    value_window = jnp.concatenate([before[1], values, after[1]], axis=0)
    position = lax.axis_index("frames")
    zero = jnp.zeros((1,), jnp.int32)
    count_pad = jnp.concatenate([zero, slab_counts, zero], axis=0)
    limits = lax.dynamic_slice_in_dim(count_pad, position, 3, 0)
    attended = attend(query, key_window, value_window, key_blocks, limits)
    whole = lax.all_gather(attended, "wshard", axis=1, tiled=True)
    mixed = split_dot(whole, o_rows)
    return mixed.astype(jnp.bfloat16)


def solution(mesh):
    return jax.shard_map(
        layer,
        mesh=mesh,
        in_specs=(
            P(("clips", "frames"), None),
            P("frames", "wshard"),
            P("frames", "wshard"),
            P("frames", "wshard"),
            P("wshard"),
            P("wshard"),
            P("frames", "wshard"),
            P(("clips", "frames"), None),
            P("clips"),
        ),
        out_specs=P(("clips", "frames"), "wshard"),
        check_vma=False,
    )
```

```python
import math

import jax
import jax.numpy as jnp
from jax import lax
from jax.experimental import pallas as pl
from jax.experimental.pallas import tpu as pltpu
from jax.sharding import PartitionSpec as P


HEAD_DIM = 128
TILE = 128


def shifted(value, axis, by):
    size = lax.axis_size(axis)
    pairs = [(i, i + by) for i in range(size) if 0 <= i + by < size]
    return lax.ppermute(value, axis, pairs)


def head_norm(raw, gain):
    rows, cols = raw.shape
    split = raw.reshape(rows, cols // HEAD_DIM, HEAD_DIM)
    square = jnp.mean(split * split, axis=-1, keepdims=True)
    normed = (split * lax.rsqrt(square + 1e-06)).reshape(rows, cols)
    return (normed * gain).astype(jnp.bfloat16)


def attend_kernel(kb_ref, lim_ref, q_ref, k_ref, v_ref, o_ref):
    tiles = q_ref.shape[0] // TILE
    picks = kb_ref.shape[1]
    scale = 1.0 / math.sqrt(HEAD_DIM)
    lanes = lax.broadcasted_iota(jnp.int32, (TILE, TILE), 1)
    rows = lax.broadcasted_iota(jnp.int32, (TILE, TILE), 0)

    def one_tile(i, carry):
        start = pl.multiple_of(i * TILE, TILE)
        q = q_ref[pl.ds(start, TILE), :]
        scores = []
        for j in range(picks):
            b = kb_ref[i, j]
            k = k_ref[pl.ds(pl.multiple_of(b * TILE, TILE), TILE), :]
            s = lax.dot_general(
                q, k, (((1,), (1,)), ((), ())), preferred_element_type=jnp.float32
            )
            s = s * scale
            slab = (b >= tiles).astype(jnp.int32) + (b >= 2 * tiles).astype(jnp.int32)
            limit = lim_ref[slab]
            pos = (b - slab * tiles) * TILE + lanes
            scores.append(jnp.where(pos < limit, s, -1e30))
        top = jnp.max(scores[0], axis=1, keepdims=True)
        for s in scores[1:]:
            top = jnp.maximum(top, jnp.max(s, axis=1, keepdims=True))
        expo = [jnp.exp(s - top) for s in scores]
        total = jnp.sum(expo[0], axis=1, keepdims=True)
        for e in expo[1:]:
            total = total + jnp.sum(e, axis=1, keepdims=True)
        acc = None
        for j in range(picks):
            b = kb_ref[i, j]
            v = v_ref[pl.ds(pl.multiple_of(b * TILE, TILE), TILE), :]
            w = (expo[j] / total).astype(jnp.bfloat16)
            part = jnp.dot(w, v, preferred_element_type=jnp.float32)
            acc = part if acc is None else acc + part
        live = start + rows < lim_ref[1]
        o_ref[pl.ds(start, TILE), :] = jnp.where(live, acc, 0.0).astype(o_ref.dtype)
        return carry

    lax.fori_loop(0, tiles, one_tile, 0)


def attend(query, keys, values, blocks, limits, interpret=False):
    rows, cols = query.shape
    window = keys.shape[0]
    heads = cols // HEAD_DIM
    spec = pltpu.PrefetchScalarGridSpec(
        num_scalar_prefetch=2,
        grid=(heads,),
        in_specs=[
            pl.BlockSpec((rows, HEAD_DIM), lambda h, kb, lim: (0, h)),
            pl.BlockSpec((window, HEAD_DIM), lambda h, kb, lim: (0, h)),
            pl.BlockSpec((window, HEAD_DIM), lambda h, kb, lim: (0, h)),
        ],
        out_specs=pl.BlockSpec((rows, HEAD_DIM), lambda h, kb, lim: (0, h)),
    )
    return pl.pallas_call(
        attend_kernel,
        grid_spec=spec,
        out_shape=jax.ShapeDtypeStruct((rows, cols), jnp.bfloat16),
        interpret=interpret,
    )(blocks.astype(jnp.int32), limits.astype(jnp.int32), query, keys, values)


def fetch(piece):
    assert lax.axis_size("clips") == 2
    ci = lax.axis_index("clips")
    share = piece.shape[1] // 2
    mine = lax.dynamic_slice_in_dim(piece, ci * share, share, 1)
    other = lax.dynamic_slice_in_dim(piece, (1 - ci) * share, share, 1)
    return lax.all_gather(mine, "frames", axis=0, tiled=True), other


def trade(fetched):
    got, other = fetched
    rows = other.shape[0]
    chunks = got.shape[0] // rows
    fi = lax.axis_index("frames")
    recv = []
    for k in range(1, chunks):
        at = (fi + k) % chunks
        part = lax.dynamic_slice_in_dim(got, at * rows, rows, 0)
        recv.append(lax.ppermute(part, "clips", [(0, 1), (1, 0)]))
    return got, other, recv


def split_dot(x, traded):
    got, other, recv = traded
    rows = other.shape[0]
    chunks = got.shape[0] // rows
    fi = lax.axis_index("frames")
    own = jnp.dot(x, got, preferred_element_type=jnp.float32)
    rest = jnp.dot(lax.dynamic_slice_in_dim(x, fi * rows, rows, 1), other,
                   preferred_element_type=jnp.float32)
    for k, part in enumerate(recv, 1):
        at = (fi + k) % chunks
        rest = rest + jnp.dot(lax.dynamic_slice_in_dim(x, at * rows, rows, 1), part,
                              preferred_element_type=jnp.float32)
    first = lax.axis_index("clips") == 0
    return jnp.where(first, jnp.concatenate([own, rest], 1), jnp.concatenate([rest, own], 1))


def layer(tokens, w_query, w_key, w_value, q_gain, k_gain, w_out, key_blocks, slab_counts):
    k_got = fetch(w_key)
    v_got = fetch(w_value)
    q_got = fetch(w_query)
    o_got = fetch(w_out)
    keys = head_norm(split_dot(tokens, trade(k_got)), k_gain)
    values = split_dot(tokens, trade(v_got)).astype(jnp.bfloat16)
    keys, values, q_got = lax.optimization_barrier((keys, values, q_got))
    query = head_norm(split_dot(tokens, trade(q_got)), q_gain)
    keys, values, o_got = lax.optimization_barrier((keys, values, o_got))
    o_rows = trade(o_got)
    before = shifted((keys, values), "frames", 1)
    after = shifted((keys, values), "frames", -1)
    key_window = jnp.concatenate([before[0], keys, after[0]], axis=0)
    value_window = jnp.concatenate([before[1], values, after[1]], axis=0)
    position = lax.axis_index("frames")
    zero = jnp.zeros((1,), jnp.int32)
    count_pad = jnp.concatenate([zero, slab_counts, zero], axis=0)
    limits = lax.dynamic_slice_in_dim(count_pad, position, 3, 0)
    attended = attend(query, key_window, value_window, key_blocks, limits)
    whole = lax.all_gather(attended, "wshard", axis=1, tiled=True)
    mixed = split_dot(whole, o_rows)
    return mixed.astype(jnp.bfloat16)


def solution(mesh):
    return jax.shard_map(
        layer,
        mesh=mesh,
        in_specs=(
            P(("clips", "frames"), None),
            P("frames", "wshard"),
            P("frames", "wshard"),
            P("frames", "wshard"),
            P("wshard"),
            P("wshard"),
            P("frames", "wshard"),
            P(("clips", "frames"), None),
            P("clips"),
        ),
        out_specs=P(("clips", "frames"), "wshard"),
        check_vma=False,
    )
```

```python
import math

import jax
import jax.numpy as jnp
from jax import lax
from jax.experimental import pallas as pl
from jax.experimental.pallas import tpu as pltpu
from jax.sharding import PartitionSpec as P


HEAD_DIM = 128
TILE = 128


def shifted(value, axis, by):
    size = lax.axis_size(axis)
    pairs = [(i, i + by) for i in range(size) if 0 <= i + by < size]
    return lax.ppermute(value, axis, pairs)


def head_norm(raw, gain):
    rows, cols = raw.shape
    split = raw.reshape(rows, cols // HEAD_DIM, HEAD_DIM)
    square = jnp.mean(split * split, axis=-1, keepdims=True)
    normed = (split * lax.rsqrt(square + 1e-06)).reshape(rows, cols)
    return (normed * gain).astype(jnp.bfloat16)


def attend_kernel(kb_ref, lim_ref, q_ref, k_ref, v_ref, o_ref):
    tiles = q_ref.shape[0] // TILE
    picks = kb_ref.shape[1]
    scale = 1.0 / math.sqrt(HEAD_DIM)
    lanes = lax.broadcasted_iota(jnp.int32, (1, TILE), 1)
    rows = lax.broadcasted_iota(jnp.int32, (TILE, 1), 0)

    def one_tile(i, carry):
        start = pl.multiple_of(i * TILE, TILE)
        q = q_ref[pl.ds(start, TILE), :]
        scores = []
        for j in range(picks):
            b = kb_ref[i, j]
            k = k_ref[pl.ds(pl.multiple_of(b * TILE, TILE), TILE), :]
            s = lax.dot_general(
                q, k, (((1,), (1,)), ((), ())), preferred_element_type=jnp.float32
            )
            s = s * scale
            slab = (b >= tiles).astype(jnp.int32) + (b >= 2 * tiles).astype(jnp.int32)
            limit = lim_ref[slab]
            pos = (b - slab * tiles) * TILE + lanes
            scores.append(jnp.where(pos < limit, s, -1e30))
        top = jnp.max(scores[0], axis=1, keepdims=True)
        for s in scores[1:]:
            top = jnp.maximum(top, jnp.max(s, axis=1, keepdims=True))
        expo = [jnp.exp(s - top) for s in scores]
        total = jnp.sum(expo[0], axis=1, keepdims=True)
        for e in expo[1:]:
            total = total + jnp.sum(e, axis=1, keepdims=True)
        inverse = 1.0 / total
        acc = None
        for j in range(picks):
            b = kb_ref[i, j]
            v = v_ref[pl.ds(pl.multiple_of(b * TILE, TILE), TILE), :]
            w = (expo[j] * inverse).astype(jnp.bfloat16)
            part = jnp.dot(w, v, preferred_element_type=jnp.float32)
            acc = part if acc is None else acc + part
        live = start + rows < lim_ref[1]
        o_ref[pl.ds(start, TILE), :] = jnp.where(live, acc, 0.0).astype(o_ref.dtype)
        return carry

    lax.fori_loop(0, tiles, one_tile, 0)


def attend(query, keys, values, blocks, limits, first=0, heads=None, interpret=False):
    rows, cols = query.shape
    window = keys.shape[0]
    if heads is None:
        heads = cols // HEAD_DIM - first
    spec = pltpu.PrefetchScalarGridSpec(
        num_scalar_prefetch=2,
        grid=(heads,),
        in_specs=[
            pl.BlockSpec((rows, HEAD_DIM), lambda h, kb, lim: (0, h + first)),
            pl.BlockSpec((window, HEAD_DIM), lambda h, kb, lim: (0, h + first)),
            pl.BlockSpec((window, HEAD_DIM), lambda h, kb, lim: (0, h + first)),
        ],
        out_specs=pl.BlockSpec((rows, HEAD_DIM), lambda h, kb, lim: (0, h)),
    )
    return pl.pallas_call(
        attend_kernel,
        grid_spec=spec,
        out_shape=jax.ShapeDtypeStruct((rows, heads * HEAD_DIM), jnp.bfloat16),
        interpret=interpret,
    )(blocks.astype(jnp.int32), limits.astype(jnp.int32), query, keys, values)


def fetch(piece):
    assert lax.axis_size("clips") == 2
    ci = lax.axis_index("clips")
    share = piece.shape[1] // 2
    mine = lax.dynamic_slice_in_dim(piece, ci * share, share, 1)
    other = lax.dynamic_slice_in_dim(piece, (1 - ci) * share, share, 1)
    return lax.all_gather(mine, "frames", axis=0, tiled=True), other


def trade(fetched):
    got, other = fetched
    rows = other.shape[0]
    chunks = got.shape[0] // rows
    fi = lax.axis_index("frames")
    recv = []
    for k in range(1, chunks):
        at = (fi + k) % chunks
        part = lax.dynamic_slice_in_dim(got, at * rows, rows, 0)
        recv.append(lax.ppermute(part, "clips", [(0, 1), (1, 0)]))
    return got, other, recv


def split_dot(x, traded):
    got, other, recv = traded
    rows = other.shape[0]
    chunks = got.shape[0] // rows
    fi = lax.axis_index("frames")
    own = jnp.dot(x, got, preferred_element_type=jnp.float32)
    rest = jnp.dot(lax.dynamic_slice_in_dim(x, fi * rows, rows, 1), other,
                   preferred_element_type=jnp.float32)
    for k, part in enumerate(recv, 1):
        at = (fi + k) % chunks
        rest = rest + jnp.dot(lax.dynamic_slice_in_dim(x, at * rows, rows, 1), part,
                              preferred_element_type=jnp.float32)
    first = lax.axis_index("clips") == 0
    return jnp.where(first, jnp.concatenate([own, rest], 1), jnp.concatenate([rest, own], 1))


def layer(tokens, w_query, w_key, w_value, q_gain, k_gain, w_out, key_blocks, slab_counts):
    k_got = fetch(w_key)
    v_got = fetch(w_value)
    q_got = fetch(w_query)
    o_got = fetch(w_out)
    keys = head_norm(split_dot(tokens, trade(k_got)), k_gain)
    values = split_dot(tokens, trade(v_got)).astype(jnp.bfloat16)
    keys, values, q_got = lax.optimization_barrier((keys, values, q_got))
    query = head_norm(split_dot(tokens, trade(q_got)), q_gain)
    keys, values, o_got = lax.optimization_barrier((keys, values, o_got))
    o_rows = trade(o_got)
    before = shifted((keys, values), "frames", 1)
    after = shifted((keys, values), "frames", -1)
    key_window = jnp.concatenate([before[0], keys, after[0]], axis=0)
    value_window = jnp.concatenate([before[1], values, after[1]], axis=0)
    position = lax.axis_index("frames")
    zero = jnp.zeros((1,), jnp.int32)
    count_pad = jnp.concatenate([zero, slab_counts, zero], axis=0)
    limits = lax.dynamic_slice_in_dim(count_pad, position, 3, 0)
    heads = query.shape[1] // HEAD_DIM
    split = heads // 2
    groups = []
    for first, count in ((0, split), (split, heads - split)):
        part = attend(query, key_window, value_window, key_blocks, limits, first, count)
        groups.append(lax.all_gather(part, "wshard", axis=1, tiled=False))
    rows = query.shape[0]
    whole = jnp.concatenate(groups, axis=2).reshape(rows, -1)
    mixed = split_dot(whole, o_rows)
    return mixed.astype(jnp.bfloat16)


def solution(mesh):
    return jax.shard_map(
        layer,
        mesh=mesh,
        in_specs=(
            P(("clips", "frames"), None),
            P("frames", "wshard"),
            P("frames", "wshard"),
            P("frames", "wshard"),
            P("wshard"),
            P("wshard"),
            P("frames", "wshard"),
            P(("clips", "frames"), None),
            P("clips"),
        ),
        out_specs=P(("clips", "frames"), "wshard"),
        check_vma=False,
    )
```

```python
import math

import jax
import jax.numpy as jnp
from jax import lax
from jax.experimental import pallas as pl
from jax.experimental.pallas import tpu as pltpu
from jax.sharding import PartitionSpec as P


HEAD_DIM = 128
TILE = 128


def shifted(value, axis, by):
    size = lax.axis_size(axis)
    pairs = [(i, i + by) for i in range(size) if 0 <= i + by < size]
    return lax.ppermute(value, axis, pairs)


def head_norm(raw, gain):
    rows, cols = raw.shape
    split = raw.reshape(rows, cols // HEAD_DIM, HEAD_DIM)
    square = jnp.mean(split * split, axis=-1, keepdims=True)
    normed = (split * lax.rsqrt(square + 1e-06)).reshape(rows, cols)
    return (normed * gain).astype(jnp.bfloat16)


def attend_kernel(kb_ref, lim_ref, q_ref, k_ref, v_ref, o_ref):
    tiles = q_ref.shape[0] // TILE
    picks = kb_ref.shape[1]
    scale = 1.0 / math.sqrt(HEAD_DIM)
    lanes = lax.broadcasted_iota(jnp.int32, (TILE, TILE), 1)
    rows = lax.broadcasted_iota(jnp.int32, (TILE, TILE), 0)

    def one_tile(i, carry):
        start = pl.multiple_of(i * TILE, TILE)
        q = q_ref[pl.ds(start, TILE), :]
        scores = []
        for j in range(picks):
            b = kb_ref[i, j]
            k = k_ref[pl.ds(pl.multiple_of(b * TILE, TILE), TILE), :]
            s = lax.dot_general(
                q, k, (((1,), (1,)), ((), ())), preferred_element_type=jnp.float32
            )
            s = s * scale
            slab = (b >= tiles).astype(jnp.int32) + (b >= 2 * tiles).astype(jnp.int32)
            limit = lim_ref[slab]
            pos = (b - slab * tiles) * TILE + lanes
            scores.append(jnp.where(pos < limit, s, -1e30))
        top = jnp.max(scores[0], axis=1, keepdims=True)
        for s in scores[1:]:
            top = jnp.maximum(top, jnp.max(s, axis=1, keepdims=True))
        expo = [jnp.exp(s - top) for s in scores]
        total = jnp.sum(expo[0], axis=1, keepdims=True)
        for e in expo[1:]:
            total = total + jnp.sum(e, axis=1, keepdims=True)
        acc = None
        for j in range(picks):
            b = kb_ref[i, j]
            v = v_ref[pl.ds(pl.multiple_of(b * TILE, TILE), TILE), :]
            w = (expo[j] / total).astype(jnp.bfloat16)
            part = jnp.dot(w, v, preferred_element_type=jnp.float32)
            acc = part if acc is None else acc + part
        live = start + rows < lim_ref[1]
        o_ref[pl.ds(start, TILE), :] = jnp.where(live, acc, 0.0).astype(o_ref.dtype)
        return carry

    lax.fori_loop(0, tiles, one_tile, 0)


def attend(query, keys, values, blocks, limits, interpret=False):
    rows, cols = query.shape
    window = keys.shape[0]
    heads = cols // HEAD_DIM
    spec = pltpu.PrefetchScalarGridSpec(
        num_scalar_prefetch=2,
        grid=(heads,),
        in_specs=[
            pl.BlockSpec((rows, HEAD_DIM), lambda h, kb, lim: (0, h)),
            pl.BlockSpec((window, HEAD_DIM), lambda h, kb, lim: (0, h)),
            pl.BlockSpec((window, HEAD_DIM), lambda h, kb, lim: (0, h)),
        ],
        out_specs=pl.BlockSpec((rows, HEAD_DIM), lambda h, kb, lim: (0, h)),
    )
    return pl.pallas_call(
        attend_kernel,
        grid_spec=spec,
        out_shape=jax.ShapeDtypeStruct((rows, cols), jnp.bfloat16),
        interpret=interpret,
    )(blocks.astype(jnp.int32), limits.astype(jnp.int32), query, keys, values)


def fetch(piece):
    assert lax.axis_size("clips") == 2
    ci = lax.axis_index("clips")
    share = piece.shape[1] // 2
    mine = lax.dynamic_slice_in_dim(piece, ci * share, share, 1)
    other = lax.dynamic_slice_in_dim(piece, (1 - ci) * share, share, 1)
    return lax.all_gather(mine, "frames", axis=0, tiled=True), other


def trade(fetched):
    got, other = fetched
    rows = other.shape[0]
    chunks = got.shape[0] // rows
    fi = lax.axis_index("frames")
    recv = []
    for k in range(1, chunks):
        at = (fi + k) % chunks
        part = lax.dynamic_slice_in_dim(got, at * rows, rows, 0)
        recv.append(lax.ppermute(part, "clips", [(0, 1), (1, 0)]))
    return got, other, recv


def split_dot(x, traded):
    got, other, recv = traded
    rows = other.shape[0]
    chunks = got.shape[0] // rows
    fi = lax.axis_index("frames")
    own = jnp.dot(x, got, preferred_element_type=jnp.float32)
    rest = jnp.dot(lax.dynamic_slice_in_dim(x, fi * rows, rows, 1), other,
                   preferred_element_type=jnp.float32)
    for k, part in enumerate(recv, 1):
        at = (fi + k) % chunks
        rest = rest + jnp.dot(lax.dynamic_slice_in_dim(x, at * rows, rows, 1), part,
                              preferred_element_type=jnp.float32)
    first = lax.axis_index("clips") == 0
    return jnp.where(first, jnp.concatenate([own, rest], 1), jnp.concatenate([rest, own], 1))


def layer(tokens, w_query, w_key, w_value, q_gain, k_gain, w_out, key_blocks, slab_counts):
    k_got = fetch(w_key)
    v_got = fetch(w_value)
    q_got = fetch(w_query)
    o_got = fetch(w_out)
    k_rows = trade(k_got)
    v_rows = trade(v_got)
    q_rows = trade(q_got)
    keys = head_norm(split_dot(tokens, k_rows), k_gain)
    values = split_dot(tokens, v_rows).astype(jnp.bfloat16)
    query = head_norm(split_dot(tokens, q_rows), q_gain)
    keys, values, o_got = lax.optimization_barrier((keys, values, o_got))
    o_rows = trade(o_got)
    position = lax.axis_index("frames")
    zero = jnp.zeros((1,), jnp.int32)
    count_pad = jnp.concatenate([zero, slab_counts, zero], axis=0)
    limits = lax.dynamic_slice_in_dim(count_pad, position, 3, 0)
    heads = query.shape[1] // HEAD_DIM
    split = heads // 2
    groups = []
    for lo, hi in ((0, split), (split, heads)):
        cols = slice(lo * HEAD_DIM, hi * HEAD_DIM)
        own = (keys[:, cols], values[:, cols])
        before = shifted(own, "frames", 1)
        after = shifted(own, "frames", -1)
        key_window = jnp.concatenate([before[0], own[0], after[0]], axis=0)
        value_window = jnp.concatenate([before[1], own[1], after[1]], axis=0)
        part = attend(query[:, cols], key_window, value_window, key_blocks, limits)
        groups.append(lax.all_gather(part, "wshard", axis=1, tiled=False))
    rows = query.shape[0]
    whole = jnp.concatenate(groups, axis=2).reshape(rows, -1)
    mixed = split_dot(whole, o_rows)
    return mixed.astype(jnp.bfloat16)


def solution(mesh):
    return jax.shard_map(
        layer,
        mesh=mesh,
        in_specs=(
            P(("clips", "frames"), None),
            P("frames", "wshard"),
            P("frames", "wshard"),
            P("frames", "wshard"),
            P("wshard"),
            P("wshard"),
            P("frames", "wshard"),
            P(("clips", "frames"), None),
            P("clips"),
        ),
        out_specs=P(("clips", "frames"), "wshard"),
        check_vma=False,
    )
```

```python
import math

import jax
import jax.numpy as jnp
from jax import lax
from jax.experimental import pallas as pl
from jax.experimental.pallas import tpu as pltpu
from jax.sharding import PartitionSpec as P


HEAD_DIM = 128
TILE = 128


def shifted(value, axis, by):
    size = lax.axis_size(axis)
    pairs = [(i, i + by) for i in range(size) if 0 <= i + by < size]
    return lax.ppermute(value, axis, pairs)


def head_norm(raw, gain):
    rows, cols = raw.shape
    split = raw.reshape(rows, cols // HEAD_DIM, HEAD_DIM)
    square = jnp.mean(split * split, axis=-1, keepdims=True)
    normed = (split * lax.rsqrt(square + 1e-06)).reshape(rows, cols)
    return (normed * gain).astype(jnp.bfloat16)


def attend_kernel(kb_ref, lim_ref, q_ref, k_ref, v_ref, o_ref):
    tiles = q_ref.shape[0] // TILE
    picks = kb_ref.shape[1]
    scale = 1.0 / math.sqrt(HEAD_DIM)
    lanes = lax.broadcasted_iota(jnp.int32, (1, TILE), 1)
    rows = lax.broadcasted_iota(jnp.int32, (TILE, 1), 0)

    def one_tile(i, carry):
        start = pl.multiple_of(i * TILE, TILE)
        q = q_ref[pl.ds(start, TILE), :]
        scores = []
        for j in range(picks):
            b = kb_ref[i, j]
            k = k_ref[pl.ds(pl.multiple_of(b * TILE, TILE), TILE), :]
            s = lax.dot_general(
                q, k, (((1,), (1,)), ((), ())), preferred_element_type=jnp.float32
            )
            s = s * scale
            slab = (b >= tiles).astype(jnp.int32) + (b >= 2 * tiles).astype(jnp.int32)
            limit = lim_ref[slab]
            pos = (b - slab * tiles) * TILE + lanes
            scores.append(jnp.where(pos < limit, s, -1e30))
        top = scores[0]
        for s in scores[1:]:
            top = jnp.maximum(top, s)
        top = jnp.max(top, axis=1, keepdims=True)
        expo = [jnp.exp(s - top) for s in scores]
        total = expo[0]
        for e in expo[1:]:
            total = total + e
        total = jnp.sum(total, axis=1, keepdims=True)
        acc = None
        for j in range(picks):
            b = kb_ref[i, j]
            v = v_ref[pl.ds(pl.multiple_of(b * TILE, TILE), TILE), :]
            w = (expo[j] / total).astype(jnp.bfloat16)
            part = jnp.dot(w, v, preferred_element_type=jnp.float32)
            acc = part if acc is None else acc + part
        live = start + rows < lim_ref[1]
        o_ref[pl.ds(start, TILE), :] = jnp.where(live, acc, 0.0).astype(o_ref.dtype)
        return carry

    lax.fori_loop(0, tiles, one_tile, 0)


def attend(query, keys, values, blocks, limits, interpret=False):
    rows, cols = query.shape
    window = keys.shape[0]
    heads = cols // HEAD_DIM
    spec = pltpu.PrefetchScalarGridSpec(
        num_scalar_prefetch=2,
        grid=(heads,),
        in_specs=[
            pl.BlockSpec((rows, HEAD_DIM), lambda h, kb, lim: (0, h)),
            pl.BlockSpec((window, HEAD_DIM), lambda h, kb, lim: (0, h)),
            pl.BlockSpec((window, HEAD_DIM), lambda h, kb, lim: (0, h)),
        ],
        out_specs=pl.BlockSpec((rows, HEAD_DIM), lambda h, kb, lim: (0, h)),
    )
    return pl.pallas_call(
        attend_kernel,
        grid_spec=spec,
        out_shape=jax.ShapeDtypeStruct((rows, cols), jnp.bfloat16),
        interpret=interpret,
    )(blocks.astype(jnp.int32), limits.astype(jnp.int32), query, keys, values)


def fetch(piece):
    assert lax.axis_size("clips") == 2
    ci = lax.axis_index("clips")
    share = piece.shape[1] // 2
    mine = lax.dynamic_slice_in_dim(piece, ci * share, share, 1)
    other = lax.dynamic_slice_in_dim(piece, (1 - ci) * share, share, 1)
    return lax.all_gather(mine, "frames", axis=0, tiled=True), other


def trade(fetched):
    got, other = fetched
    rows = other.shape[0]
    chunks = got.shape[0] // rows
    fi = lax.axis_index("frames")
    recv = []
    for k in range(1, chunks):
        at = (fi + k) % chunks
        part = lax.dynamic_slice_in_dim(got, at * rows, rows, 0)
        recv.append(lax.ppermute(part, "clips", [(0, 1), (1, 0)]))
    return got, other, recv


def split_dot(x, traded):
    got, other, recv = traded
    rows = other.shape[0]
    chunks = got.shape[0] // rows
    fi = lax.axis_index("frames")
    own = jnp.dot(x, got, preferred_element_type=jnp.float32)
    rest = jnp.dot(lax.dynamic_slice_in_dim(x, fi * rows, rows, 1), other,
                   preferred_element_type=jnp.float32)
    for k, part in enumerate(recv, 1):
        at = (fi + k) % chunks
        rest = rest + jnp.dot(lax.dynamic_slice_in_dim(x, at * rows, rows, 1), part,
                              preferred_element_type=jnp.float32)
    first = lax.axis_index("clips") == 0
    return jnp.where(first, jnp.concatenate([own, rest], 1), jnp.concatenate([rest, own], 1))


def layer(tokens, w_query, w_key, w_value, q_gain, k_gain, w_out, key_blocks, slab_counts):
    k_got = fetch(w_key)
    v_got = fetch(w_value)
    q_got = fetch(w_query)
    o_got = fetch(w_out)
    keys = head_norm(split_dot(tokens, trade(k_got)), k_gain)
    values = split_dot(tokens, trade(v_got)).astype(jnp.bfloat16)
    keys, values, q_got = lax.optimization_barrier((keys, values, q_got))
    query = head_norm(split_dot(tokens, trade(q_got)), q_gain)
    keys, values, o_got = lax.optimization_barrier((keys, values, o_got))
    o_rows = trade(o_got)
    before = shifted((keys, values), "frames", 1)
    after = shifted((keys, values), "frames", -1)
    key_window = jnp.concatenate([before[0], keys, after[0]], axis=0)
    value_window = jnp.concatenate([before[1], values, after[1]], axis=0)
    position = lax.axis_index("frames")
    zero = jnp.zeros((1,), jnp.int32)
    count_pad = jnp.concatenate([zero, slab_counts, zero], axis=0)
    limits = lax.dynamic_slice_in_dim(count_pad, position, 3, 0)
    attended = attend(query, key_window, value_window, key_blocks, limits)
    whole = lax.all_gather(attended, "wshard", axis=1, tiled=True)
    mixed = split_dot(whole, o_rows)
    return mixed.astype(jnp.bfloat16)


def solution(mesh):
    return jax.shard_map(
        layer,
        mesh=mesh,
        in_specs=(
            P(("clips", "frames"), None),
            P("frames", "wshard"),
            P("frames", "wshard"),
            P("frames", "wshard"),
            P("wshard"),
            P("wshard"),
            P("frames", "wshard"),
            P(("clips", "frames"), None),
            P("clips"),
        ),
        out_specs=P(("clips", "frames"), "wshard"),
        check_vma=False,
    )
```

```python
import functools
import math

import jax
import jax.numpy as jnp
from jax import lax
from jax.experimental import pallas as pl
from jax.experimental.pallas import tpu as pltpu
from jax.sharding import PartitionSpec as P


HEAD_DIM = 128
TILE = 128


def shifted(value, axis, by):
    size = lax.axis_size(axis)
    pairs = [(i, i + by) for i in range(size) if 0 <= i + by < size]
    return lax.ppermute(value, axis, pairs)


def head_norm(raw, gain):
    rows, cols = raw.shape
    split = raw.reshape(rows, cols // HEAD_DIM, HEAD_DIM)
    square = jnp.mean(split * split, axis=-1, keepdims=True)
    normed = (split * lax.rsqrt(square + 1e-06)).reshape(rows, cols)
    return (normed * gain).astype(jnp.bfloat16)


def attend_kernel(kb_ref, lim_ref, q_ref, k_ref, v_ref, o_ref, *, first_tile):
    tiles = q_ref.shape[0] // TILE
    slab_tiles = k_ref.shape[0] // (3 * TILE)
    picks = kb_ref.shape[1]
    scale = 1.0 / math.sqrt(HEAD_DIM)
    lanes = lax.broadcasted_iota(jnp.int32, (1, TILE), 1)
    rows = lax.broadcasted_iota(jnp.int32, (TILE, 1), 0)

    def one_tile(i, carry):
        start = pl.multiple_of(i * TILE, TILE)
        q = q_ref[pl.ds(start, TILE), :]
        scores = []
        for j in range(picks):
            b = kb_ref[i, j]
            k = k_ref[pl.ds(pl.multiple_of(b * TILE, TILE), TILE), :]
            s = lax.dot_general(
                q, k, (((1,), (1,)), ((), ())), preferred_element_type=jnp.float32
            )
            slab = (b >= slab_tiles).astype(jnp.int32) + (b >= 2 * slab_tiles).astype(jnp.int32)
            limit = lim_ref[slab]
            pos = (b - slab * slab_tiles) * TILE + lanes
            scores.append(jnp.where(pos < limit, s, -1e30))
        top = scores[0]
        for s in scores[1:]:
            top = jnp.maximum(top, s)
        top = jnp.max(top, axis=1, keepdims=True)
        expo = [jnp.exp((s - top) * scale) for s in scores]
        total = expo[0]
        for e in expo[1:]:
            total = total + e
        total = jnp.sum(total, axis=1, keepdims=True)
        acc = None
        for j in range(picks):
            b = kb_ref[i, j]
            v = v_ref[pl.ds(pl.multiple_of(b * TILE, TILE), TILE), :]
            w = (expo[j] / total).astype(jnp.bfloat16)
            part = jnp.dot(w, v, preferred_element_type=jnp.float32)
            acc = part if acc is None else acc + part
        live = (i + first_tile) * TILE + rows < lim_ref[1]
        o_ref[pl.ds(start, TILE), :] = jnp.where(live, acc, 0.0).astype(o_ref.dtype)
        return carry

    lax.fori_loop(0, tiles, one_tile, 0)


def attend(query, keys, values, blocks, limits, first_tile=0, interpret=False):
    rows, cols = query.shape
    window = keys.shape[0]
    heads = cols // HEAD_DIM
    spec = pltpu.PrefetchScalarGridSpec(
        num_scalar_prefetch=2,
        grid=(heads,),
        in_specs=[
            pl.BlockSpec((rows, HEAD_DIM), lambda h, kb, lim: (0, h)),
            pl.BlockSpec((window, HEAD_DIM), lambda h, kb, lim: (0, h)),
            pl.BlockSpec((window, HEAD_DIM), lambda h, kb, lim: (0, h)),
        ],
        out_specs=pl.BlockSpec((rows, HEAD_DIM), lambda h, kb, lim: (0, h)),
    )
    return pl.pallas_call(
        functools.partial(attend_kernel, first_tile=first_tile),
        grid_spec=spec,
        out_shape=jax.ShapeDtypeStruct((rows, cols), jnp.bfloat16),
        interpret=interpret,
    )(blocks.astype(jnp.int32), limits.astype(jnp.int32), query, keys, values)


def fetch(piece):
    assert lax.axis_size("clips") == 2
    ci = lax.axis_index("clips")
    share = piece.shape[1] // 2
    mine = lax.dynamic_slice_in_dim(piece, ci * share, share, 1)
    other = lax.dynamic_slice_in_dim(piece, (1 - ci) * share, share, 1)
    return lax.all_gather(mine, "frames", axis=0, tiled=True), other


def trade(fetched):
    got, other = fetched
    rows = other.shape[0]
    chunks = got.shape[0] // rows
    fi = lax.axis_index("frames")
    recv = []
    for k in range(1, chunks):
        at = (fi + k) % chunks
        part = lax.dynamic_slice_in_dim(got, at * rows, rows, 0)
        recv.append(lax.ppermute(part, "clips", [(0, 1), (1, 0)]))
    return got, other, recv


def split_dot(x, traded):
    got, other, recv = traded
    rows = other.shape[0]
    chunks = got.shape[0] // rows
    fi = lax.axis_index("frames")
    own = jnp.dot(x, got, preferred_element_type=jnp.float32)
    rest = jnp.dot(lax.dynamic_slice_in_dim(x, fi * rows, rows, 1), other,
                   preferred_element_type=jnp.float32)
    for k, part in enumerate(recv, 1):
        at = (fi + k) % chunks
        rest = rest + jnp.dot(lax.dynamic_slice_in_dim(x, at * rows, rows, 1), part,
                              preferred_element_type=jnp.float32)
    first = lax.axis_index("clips") == 0
    return jnp.where(first, jnp.concatenate([own, rest], 1), jnp.concatenate([rest, own], 1))


def layer(tokens, w_query, w_key, w_value, q_gain, k_gain, w_out, key_blocks, slab_counts):
    k_got = fetch(w_key)
    v_got = fetch(w_value)
    q_got = fetch(w_query)
    o_got = fetch(w_out)
    keys = head_norm(split_dot(tokens, trade(k_got)), k_gain)
    values = split_dot(tokens, trade(v_got)).astype(jnp.bfloat16)
    keys, values, q_got = lax.optimization_barrier((keys, values, q_got))
    query = head_norm(split_dot(tokens, trade(q_got)), q_gain)
    keys, values, o_got = lax.optimization_barrier((keys, values, o_got))
    o_rows = trade(o_got)
    before = shifted((keys, values), "frames", 1)
    after = shifted((keys, values), "frames", -1)
    key_window = jnp.concatenate([before[0], keys, after[0]], axis=0)
    value_window = jnp.concatenate([before[1], values, after[1]], axis=0)
    position = lax.axis_index("frames")
    zero = jnp.zeros((1,), jnp.int32)
    count_pad = jnp.concatenate([zero, slab_counts, zero], axis=0)
    limits = lax.dynamic_slice_in_dim(count_pad, position, 3, 0)
    tiles = query.shape[0] // TILE
    half = tiles // 2
    mixed = []
    for lo, hi in ((0, half), (half, tiles)):
        part = attend(query[lo * TILE:hi * TILE], key_window, value_window,
                      key_blocks[lo:hi], limits, lo)
        whole = lax.all_gather(part, "wshard", axis=1, tiled=True)
        mixed.append(split_dot(whole, o_rows).astype(jnp.bfloat16))
    return jnp.concatenate(mixed, axis=0)


def solution(mesh):
    return jax.shard_map(
        layer,
        mesh=mesh,
        in_specs=(
            P(("clips", "frames"), None),
            P("frames", "wshard"),
            P("frames", "wshard"),
            P("frames", "wshard"),
            P("wshard"),
            P("wshard"),
            P("frames", "wshard"),
            P(("clips", "frames"), None),
            P("clips"),
        ),
        out_specs=P(("clips", "frames"), "wshard"),
        check_vma=False,
    )
```

```python
import functools
import math

import jax
import jax.numpy as jnp
from jax import lax
from jax.experimental import pallas as pl
from jax.experimental.pallas import tpu as pltpu
from jax.sharding import PartitionSpec as P


HEAD_DIM = 128
TILE = 128


def shifted(value, axis, by):
    size = lax.axis_size(axis)
    pairs = [(i, i + by) for i in range(size) if 0 <= i + by < size]
    return lax.ppermute(value, axis, pairs)


def head_norm(raw, gain):
    rows, cols = raw.shape
    split = raw.reshape(rows, cols // HEAD_DIM, HEAD_DIM)
    square = jnp.mean(split * split, axis=-1, keepdims=True)
    normed = (split * lax.rsqrt(square + 1e-06)).reshape(rows, cols)
    return (normed * gain).astype(jnp.bfloat16)


def attend_kernel(kb_ref, lim_ref, q_ref, k0, k1, k2, v0, v1, v2, o_ref, *, first_tile):
    def load(refs, b):
        slab = (b >= slab_tiles).astype(jnp.int32) + (b >= 2 * slab_tiles).astype(jnp.int32)
        at = pl.ds(pl.multiple_of((b - slab * slab_tiles) * TILE, TILE), TILE)
        return lax.cond(
            slab == 1,
            lambda: refs[1][at, :],
            lambda: lax.cond(slab == 0, lambda: refs[0][at, :], lambda: refs[2][at, :]),
        )

    tiles = q_ref.shape[0] // TILE
    slab_tiles = k0.shape[0] // TILE
    picks = kb_ref.shape[1]
    scale = 1.0 / math.sqrt(HEAD_DIM)
    lanes = lax.broadcasted_iota(jnp.int32, (1, TILE), 1)
    rows = lax.broadcasted_iota(jnp.int32, (TILE, 1), 0)

    def one_tile(i, carry):
        start = pl.multiple_of(i * TILE, TILE)
        q = q_ref[pl.ds(start, TILE), :]
        scores = []
        for j in range(picks):
            b = kb_ref[i, j]
            k = load((k0, k1, k2), b)
            s = lax.dot_general(
                q, k, (((1,), (1,)), ((), ())), preferred_element_type=jnp.float32
            )
            slab = (b >= slab_tiles).astype(jnp.int32) + (b >= 2 * slab_tiles).astype(jnp.int32)
            limit = lim_ref[slab]
            pos = (b - slab * slab_tiles) * TILE + lanes
            scores.append(jnp.where(pos < limit, s, -1e30))
        top = scores[0]
        for s in scores[1:]:
            top = jnp.maximum(top, s)
        top = jnp.max(top, axis=1, keepdims=True)
        expo = [jnp.exp((s - top) * scale) for s in scores]
        total = expo[0]
        for e in expo[1:]:
            total = total + e
        total = jnp.sum(total, axis=1, keepdims=True)
        acc = None
        for j in range(picks):
            b = kb_ref[i, j]
            v = load((v0, v1, v2), b)
            w = (expo[j] / total).astype(jnp.bfloat16)
            part = jnp.dot(w, v, preferred_element_type=jnp.float32)
            acc = part if acc is None else acc + part
        live = (i + first_tile) * TILE + rows < lim_ref[1]
        o_ref[pl.ds(start, TILE), :] = jnp.where(live, acc, 0.0).astype(o_ref.dtype)
        return carry

    lax.fori_loop(0, tiles, one_tile, 0)


def attend(query, keys, values, blocks, limits, first_tile=0, interpret=False):
    rows, cols = query.shape
    window = keys[0].shape[0]
    heads = cols // HEAD_DIM
    spec = pltpu.PrefetchScalarGridSpec(
        num_scalar_prefetch=2,
        grid=(heads,),
        in_specs=[
            pl.BlockSpec((rows, HEAD_DIM), lambda h, kb, lim: (0, h)),
        ] + [pl.BlockSpec((window, HEAD_DIM), lambda h, kb, lim: (0, h))] * 6,
        out_specs=pl.BlockSpec((rows, HEAD_DIM), lambda h, kb, lim: (0, h)),
    )
    return pl.pallas_call(
        functools.partial(attend_kernel, first_tile=first_tile),
        grid_spec=spec,
        out_shape=jax.ShapeDtypeStruct((rows, cols), jnp.bfloat16),
        interpret=interpret,
    )(blocks.astype(jnp.int32), limits.astype(jnp.int32), query, *keys, *values)


def fetch(piece):
    assert lax.axis_size("clips") == 2
    ci = lax.axis_index("clips")
    share = piece.shape[1] // 2
    mine = lax.dynamic_slice_in_dim(piece, ci * share, share, 1)
    other = lax.dynamic_slice_in_dim(piece, (1 - ci) * share, share, 1)
    return lax.all_gather(mine, "frames", axis=0, tiled=True), other


def trade(fetched):
    got, other = fetched
    rows = other.shape[0]
    chunks = got.shape[0] // rows
    fi = lax.axis_index("frames")
    recv = []
    for k in range(1, chunks):
        at = (fi + k) % chunks
        part = lax.dynamic_slice_in_dim(got, at * rows, rows, 0)
        recv.append(lax.ppermute(part, "clips", [(0, 1), (1, 0)]))
    return got, other, recv


def split_dot(x, traded):
    got, other, recv = traded
    rows = other.shape[0]
    chunks = got.shape[0] // rows
    fi = lax.axis_index("frames")
    own = jnp.dot(x, got, preferred_element_type=jnp.float32)
    rest = jnp.dot(lax.dynamic_slice_in_dim(x, fi * rows, rows, 1), other,
                   preferred_element_type=jnp.float32)
    for k, part in enumerate(recv, 1):
        at = (fi + k) % chunks
        rest = rest + jnp.dot(lax.dynamic_slice_in_dim(x, at * rows, rows, 1), part,
                              preferred_element_type=jnp.float32)
    first = lax.axis_index("clips") == 0
    return jnp.where(first, jnp.concatenate([own, rest], 1), jnp.concatenate([rest, own], 1))


def layer(tokens, w_query, w_key, w_value, q_gain, k_gain, w_out, key_blocks, slab_counts):
    k_got = fetch(w_key)
    v_got = fetch(w_value)
    q_got = fetch(w_query)
    o_got = fetch(w_out)
    keys = head_norm(split_dot(tokens, trade(k_got)), k_gain)
    values = split_dot(tokens, trade(v_got)).astype(jnp.bfloat16)
    keys, values, q_got = lax.optimization_barrier((keys, values, q_got))
    query = head_norm(split_dot(tokens, trade(q_got)), q_gain)
    keys, values, o_got = lax.optimization_barrier((keys, values, o_got))
    o_rows = trade(o_got)
    before = shifted((keys, values), "frames", 1)
    after = shifted((keys, values), "frames", -1)
    key_window = (before[0], keys, after[0])
    value_window = (before[1], values, after[1])
    position = lax.axis_index("frames")
    zero = jnp.zeros((1,), jnp.int32)
    count_pad = jnp.concatenate([zero, slab_counts, zero], axis=0)
    limits = lax.dynamic_slice_in_dim(count_pad, position, 3, 0)
    tiles = query.shape[0] // TILE
    half = tiles // 2
    mixed = []
    for lo, hi in ((0, half), (half, tiles)):
        part = attend(query[lo * TILE:hi * TILE], key_window, value_window,
                      key_blocks[lo:hi], limits, lo)
        whole = lax.all_gather(part, "wshard", axis=1, tiled=True)
        mixed.append(split_dot(whole, o_rows).astype(jnp.bfloat16))
    return jnp.concatenate(mixed, axis=0)


def solution(mesh):
    return jax.shard_map(
        layer,
        mesh=mesh,
        in_specs=(
            P(("clips", "frames"), None),
            P("frames", "wshard"),
            P("frames", "wshard"),
            P("frames", "wshard"),
            P("wshard"),
            P("wshard"),
            P("frames", "wshard"),
            P(("clips", "frames"), None),
            P("clips"),
        ),
        out_specs=P(("clips", "frames"), "wshard"),
        check_vma=False,
    )
```

```python
import functools
import math

import jax
import jax.numpy as jnp
from jax import lax
from jax.experimental import pallas as pl
from jax.experimental.pallas import tpu as pltpu
from jax.sharding import PartitionSpec as P


HEAD_DIM = 128
TILE = 128


def shifted(value, axis, by):
    size = lax.axis_size(axis)
    pairs = [(i, i + by) for i in range(size) if 0 <= i + by < size]
    return lax.ppermute(value, axis, pairs)


def head_norm(raw, gain):
    rows, cols = raw.shape
    split = raw.reshape(rows, cols // HEAD_DIM, HEAD_DIM)
    square = jnp.mean(split * split, axis=-1, keepdims=True)
    normed = (split * lax.rsqrt(square + 1e-06)).reshape(rows, cols)
    return (normed * gain).astype(jnp.bfloat16)


def attend_kernel(kb_ref, lim_ref, q_ref, k_ref, v_ref, o_ref, *, first_tile):
    tiles = q_ref.shape[0] // TILE
    slab_tiles = k_ref.shape[0] // (3 * TILE)
    picks = kb_ref.shape[1]
    scale = 1.0 / math.sqrt(HEAD_DIM)
    lanes = lax.broadcasted_iota(jnp.int32, (1, TILE), 1)
    rows = lax.broadcasted_iota(jnp.int32, (TILE, 1), 0)

    def one_tile(i, carry):
        start = pl.multiple_of(i * TILE, TILE)
        q = q_ref[pl.ds(start, TILE), :]
        scores = []
        for j in range(picks):
            b = kb_ref[i, j]
            k = k_ref[pl.ds(pl.multiple_of(b * TILE, TILE), TILE), :]
            s = lax.dot_general(
                q, k, (((1,), (1,)), ((), ())), preferred_element_type=jnp.float32
            )
            s = s * scale
            slab = (b >= slab_tiles).astype(jnp.int32) + (b >= 2 * slab_tiles).astype(jnp.int32)
            limit = lim_ref[slab]
            pos = (b - slab * slab_tiles) * TILE + lanes
            scores.append(jnp.where(pos < limit, s, -1e30))
        top = scores[0]
        for s in scores[1:]:
            top = jnp.maximum(top, s)
        top = jnp.max(top, axis=1, keepdims=True)
        expo = [jnp.exp(s - top) for s in scores]
        total = expo[0]
        for e in expo[1:]:
            total = total + e
        total = jnp.sum(total, axis=1, keepdims=True)
        acc = None
        for j in range(picks):
            b = kb_ref[i, j]
            v = v_ref[pl.ds(pl.multiple_of(b * TILE, TILE), TILE), :]
            w = (expo[j] / total).astype(jnp.bfloat16)
            part = jnp.dot(w, v, preferred_element_type=jnp.float32)
            acc = part if acc is None else acc + part
        live = (i + first_tile) * TILE + rows < lim_ref[1]
        o_ref[pl.ds(start, TILE), :] = jnp.where(live, acc, 0.0).astype(o_ref.dtype)
        return carry

    lax.fori_loop(0, tiles, one_tile, 0)


def attend(query, keys, values, blocks, limits, first_tile=0, interpret=False):
    rows, cols = query.shape
    window = keys.shape[0]
    heads = cols // HEAD_DIM
    spec = pltpu.PrefetchScalarGridSpec(
        num_scalar_prefetch=2,
        grid=(heads,),
        in_specs=[
            pl.BlockSpec((rows, HEAD_DIM), lambda h, kb, lim: (0, h)),
            pl.BlockSpec((window, HEAD_DIM), lambda h, kb, lim: (0, h)),
            pl.BlockSpec((window, HEAD_DIM), lambda h, kb, lim: (0, h)),
        ],
        out_specs=pl.BlockSpec((rows, HEAD_DIM), lambda h, kb, lim: (0, h)),
    )
    return pl.pallas_call(
        functools.partial(attend_kernel, first_tile=first_tile),
        grid_spec=spec,
        out_shape=jax.ShapeDtypeStruct((rows, cols), jnp.bfloat16),
        interpret=interpret,
    )(blocks.astype(jnp.int32), limits.astype(jnp.int32), query, keys, values)


def fetch(piece):
    assert lax.axis_size("clips") == 2
    ci = lax.axis_index("clips")
    share = piece.shape[1] // 2
    mine = lax.dynamic_slice_in_dim(piece, ci * share, share, 1)
    other = lax.dynamic_slice_in_dim(piece, (1 - ci) * share, share, 1)
    return lax.all_gather(mine, "frames", axis=0, tiled=True), other


def trade(fetched):
    got, other = fetched
    rows = other.shape[0]
    chunks = got.shape[0] // rows
    fi = lax.axis_index("frames")
    recv = []
    for k in range(1, chunks):
        at = (fi + k) % chunks
        part = lax.dynamic_slice_in_dim(got, at * rows, rows, 0)
        recv.append(lax.ppermute(part, "clips", [(0, 1), (1, 0)]))
    return got, other, recv


def split_dot(x, traded):
    got, other, recv = traded
    rows = other.shape[0]
    chunks = got.shape[0] // rows
    fi = lax.axis_index("frames")
    own = jnp.dot(x, got, preferred_element_type=jnp.float32)
    rest = jnp.dot(lax.dynamic_slice_in_dim(x, fi * rows, rows, 1), other,
                   preferred_element_type=jnp.float32)
    for k, part in enumerate(recv, 1):
        at = (fi + k) % chunks
        rest = rest + jnp.dot(lax.dynamic_slice_in_dim(x, at * rows, rows, 1), part,
                              preferred_element_type=jnp.float32)
    first = lax.axis_index("clips") == 0
    return jnp.where(first, jnp.concatenate([own, rest], 1), jnp.concatenate([rest, own], 1))


def layer(tokens, w_query, w_key, w_value, q_gain, k_gain, w_out, key_blocks, slab_counts):
    k_got = fetch(w_key)
    v_got = fetch(w_value)
    q_got = fetch(w_query)
    o_got = fetch(w_out)
    keys = head_norm(split_dot(tokens, trade(k_got)), k_gain)
    values = split_dot(tokens, trade(v_got)).astype(jnp.bfloat16)
    keys, values, q_got = lax.optimization_barrier((keys, values, q_got))
    query = head_norm(split_dot(tokens, trade(q_got)), q_gain)
    width = keys.shape[1]
    both, o_got = lax.optimization_barrier((jnp.concatenate([keys, values], axis=1), o_got))
    keys, values = both[:, :width], both[:, width:]
    o_rows = trade(o_got)
    before = shifted(both, "frames", 1)
    after = shifted(both, "frames", -1)
    key_window = jnp.concatenate([before[:, :width], keys, after[:, :width]], axis=0)
    value_window = jnp.concatenate([before[:, width:], values, after[:, width:]], axis=0)
    position = lax.axis_index("frames")
    zero = jnp.zeros((1,), jnp.int32)
    count_pad = jnp.concatenate([zero, slab_counts, zero], axis=0)
    limits = lax.dynamic_slice_in_dim(count_pad, position, 3, 0)
    tiles = query.shape[0] // TILE
    half = tiles // 3
    mixed = []
    for lo, hi in ((0, half), (half, tiles)):
        part = attend(query[lo * TILE:hi * TILE], key_window, value_window,
                      key_blocks[lo:hi], limits, lo)
        whole = lax.all_gather(part, "wshard", axis=1, tiled=True)
        mixed.append(split_dot(whole, o_rows).astype(jnp.bfloat16))
    return jnp.concatenate(mixed, axis=0)


def solution(mesh):
    return jax.shard_map(
        layer,
        mesh=mesh,
        in_specs=(
            P(("clips", "frames"), None),
            P("frames", "wshard"),
            P("frames", "wshard"),
            P("frames", "wshard"),
            P("wshard"),
            P("wshard"),
            P("frames", "wshard"),
            P(("clips", "frames"), None),
            P("clips"),
        ),
        out_specs=P(("clips", "frames"), "wshard"),
        check_vma=False,
    )
```

```python
import functools
import math

import jax
import jax.numpy as jnp
from jax import lax
from jax.experimental import pallas as pl
from jax.experimental.pallas import tpu as pltpu
from jax.sharding import PartitionSpec as P


HEAD_DIM = 128
TILE = 128


def shifted(value, axis, by):
    size = lax.axis_size(axis)
    pairs = [(i, i + by) for i in range(size) if 0 <= i + by < size]
    return lax.ppermute(value, axis, pairs)


def head_norm(raw, gain):
    rows, cols = raw.shape
    split = raw.reshape(rows, cols // HEAD_DIM, HEAD_DIM)
    square = jnp.mean(split * split, axis=-1, keepdims=True)
    normed = (split * lax.rsqrt(square + 1e-06)).reshape(rows, cols)
    return (normed * gain).astype(jnp.bfloat16)


def attend_kernel(kb_ref, lim_ref, q_ref, k_ref, v_ref, o_ref, *, first_tile):
    tiles = q_ref.shape[0] // TILE
    slab_tiles = k_ref.shape[0] // (3 * TILE)
    picks = kb_ref.shape[1]
    scale = 1.0 / math.sqrt(HEAD_DIM)
    lanes = lax.broadcasted_iota(jnp.int32, (1, TILE), 1)
    rows = lax.broadcasted_iota(jnp.int32, (TILE, 1), 0)

    def one_tile(i, carry):
        start = pl.multiple_of(i * TILE, TILE)
        q = q_ref[pl.ds(start, TILE), :]
        scores = []
        for j in range(picks):
            b = kb_ref[i, j]
            k = k_ref[pl.ds(pl.multiple_of(b * TILE, TILE), TILE), :]
            s = lax.dot_general(
                q, k, (((1,), (1,)), ((), ())), preferred_element_type=jnp.float32
            )
            s = s * scale
            slab = (b >= slab_tiles).astype(jnp.int32) + (b >= 2 * slab_tiles).astype(jnp.int32)
            limit = lim_ref[slab]
            pos = (b - slab * slab_tiles) * TILE + lanes
            scores.append(jnp.where(pos < limit, s, -1e30))
        top = scores[0]
        for s in scores[1:]:
            top = jnp.maximum(top, s)
        top = jnp.max(top, axis=1, keepdims=True)
        expo = [jnp.exp(s - top) for s in scores]
        total = expo[0]
        for e in expo[1:]:
            total = total + e
        total = jnp.sum(total, axis=1, keepdims=True)
        acc = None
        for j in range(picks):
            b = kb_ref[i, j]
            v = v_ref[pl.ds(pl.multiple_of(b * TILE, TILE), TILE), :]
            w = (expo[j] / total).astype(jnp.bfloat16)
            part = jnp.dot(w, v, preferred_element_type=jnp.float32)
            acc = part if acc is None else acc + part
        live = (i + first_tile) * TILE + rows < lim_ref[1]
        o_ref[pl.ds(start, TILE), :] = jnp.where(live, acc, 0.0).astype(o_ref.dtype)
        return carry

    lax.fori_loop(0, tiles, one_tile, 0, unroll=True)


def attend(query, keys, values, blocks, limits, first_tile=0, interpret=False):
    rows, cols = query.shape
    window = keys.shape[0]
    heads = cols // HEAD_DIM
    spec = pltpu.PrefetchScalarGridSpec(
        num_scalar_prefetch=2,
        grid=(heads,),
        in_specs=[
            pl.BlockSpec((rows, HEAD_DIM), lambda h, kb, lim: (0, h)),
            pl.BlockSpec((window, HEAD_DIM), lambda h, kb, lim: (0, h)),
            pl.BlockSpec((window, HEAD_DIM), lambda h, kb, lim: (0, h)),
        ],
        out_specs=pl.BlockSpec((rows, HEAD_DIM), lambda h, kb, lim: (0, h)),
    )
    return pl.pallas_call(
        functools.partial(attend_kernel, first_tile=first_tile),
        grid_spec=spec,
        out_shape=jax.ShapeDtypeStruct((rows, cols), jnp.bfloat16),
        interpret=interpret,
    )(blocks.astype(jnp.int32), limits.astype(jnp.int32), query, keys, values)


def fetch(piece):
    assert lax.axis_size("clips") == 2
    ci = lax.axis_index("clips")
    share = piece.shape[1] // 2
    mine = lax.dynamic_slice_in_dim(piece, ci * share, share, 1)
    other = lax.dynamic_slice_in_dim(piece, (1 - ci) * share, share, 1)
    return lax.all_gather(mine, "frames", axis=0, tiled=True), other


def trade(fetched):
    got, other = fetched
    rows = other.shape[0]
    chunks = got.shape[0] // rows
    fi = lax.axis_index("frames")
    recv = []
    for k in range(1, chunks):
        at = (fi + k) % chunks
        part = lax.dynamic_slice_in_dim(got, at * rows, rows, 0)
        recv.append(lax.ppermute(part, "clips", [(0, 1), (1, 0)]))
    return got, other, recv


def split_dot(x, traded):
    got, other, recv = traded
    rows = other.shape[0]
    chunks = got.shape[0] // rows
    fi = lax.axis_index("frames")
    own = jnp.dot(x, got, preferred_element_type=jnp.float32)
    rest = jnp.dot(lax.dynamic_slice_in_dim(x, fi * rows, rows, 1), other,
                   preferred_element_type=jnp.float32)
    for k, part in enumerate(recv, 1):
        at = (fi + k) % chunks
        rest = rest + jnp.dot(lax.dynamic_slice_in_dim(x, at * rows, rows, 1), part,
                              preferred_element_type=jnp.float32)
    first = lax.axis_index("clips") == 0
    return jnp.where(first, jnp.concatenate([own, rest], 1), jnp.concatenate([rest, own], 1))


def layer(tokens, w_query, w_key, w_value, q_gain, k_gain, w_out, key_blocks, slab_counts):
    k_got = fetch(w_key)
    v_got = fetch(w_value)
    q_got = fetch(w_query)
    o_got = fetch(w_out)
    keys = head_norm(split_dot(tokens, trade(k_got)), k_gain)
    values = split_dot(tokens, trade(v_got)).astype(jnp.bfloat16)
    keys, values, q_got = lax.optimization_barrier((keys, values, q_got))
    query = head_norm(split_dot(tokens, trade(q_got)), q_gain)
    keys, values, o_got = lax.optimization_barrier((keys, values, o_got))
    o_rows = trade(o_got)
    both = jnp.concatenate([keys, values], axis=1)
    width = keys.shape[1]
    before = shifted(both, "frames", 1)
    after = shifted(both, "frames", -1)
    key_window = jnp.concatenate([before[:, :width], keys, after[:, :width]], axis=0)
    value_window = jnp.concatenate([before[:, width:], values, after[:, width:]], axis=0)
    position = lax.axis_index("frames")
    zero = jnp.zeros((1,), jnp.int32)
    count_pad = jnp.concatenate([zero, slab_counts, zero], axis=0)
    limits = lax.dynamic_slice_in_dim(count_pad, position, 3, 0)
    tiles = query.shape[0] // TILE
    half = tiles // 2
    mixed = []
    for lo, hi in ((0, half), (half, tiles)):
        part = attend(query[lo * TILE:hi * TILE], key_window, value_window,
                      key_blocks[lo:hi], limits, lo)
        whole = lax.all_gather(part, "wshard", axis=1, tiled=True)
        mixed.append(split_dot(whole, o_rows).astype(jnp.bfloat16))
    return jnp.concatenate(mixed, axis=0)


def solution(mesh):
    return jax.shard_map(
        layer,
        mesh=mesh,
        in_specs=(
            P(("clips", "frames"), None),
            P("frames", "wshard"),
            P("frames", "wshard"),
            P("frames", "wshard"),
            P("wshard"),
            P("wshard"),
            P("frames", "wshard"),
            P(("clips", "frames"), None),
            P("clips"),
        ),
        out_specs=P(("clips", "frames"), "wshard"),
        check_vma=False,
    )
```
